32 devices in a mesh: gx: 2 (over core), gy: 4 (over y, x), gz: 4 (over z).
Axes of the slice: x: 2, y: 2, z: 4, core: 2. Of those that a mesh axis runs over, the one named last changes fastest.
Arguments:
- labels: int32 [16, 32, 512], P('gx', 'gy', 'gz'), may hold values from 0 to 3, as said below
- mu_start: float32 [2, 16, 32, 512], P(None, 'gx', 'gy', 'gz'), may hold values from -4 to 4
- front_blocks: int32 [32, 3], replicated, may hold values from 0 to 26, as said below
Outputs:
- phases: float32 [4, 16, 32, 512], P(None, 'gx', 'gy', 'gz')
- potentials: float32 [2, 16, 32, 512], P(None, 'gx', 'gy', 'gz')
The draws below stay inside these ranges and needn't reach their ends.
Inputs may be any that keep to these rules, and one draw needn't show every extreme that they name: `front_blocks`: each row is (x brick, y brick, z block) of one block; no block is listed twice; each lateral brick column has 4 rows with consecutive z blocks; the z blocks lie from 4 // 2 * (8) to (4 // 2 + 1) * 8 + 2, and the first blocks of all columns lie within 8 blocks of one another; one brick of 8 x 8 x 128 cells holds at most 4 listed blocks, and some brick holds exactly 4. `labels`: 0 is liquid, 1 to 3 the solids; in each lateral column the cells below a front height are solid and those above it liquid, and the front height lies inside that column's listed blocks.
All inputs are finite; a program needn't handle non-finite values.
Results may differ from the reference program's by a relative error of at most 0.00002.
Values sent between devices are 32-bit elements; how exact they have to be, the bound alone decides.
No kernel may reach another device: no remote copies, remote signals or barrier semaphores. Data moves between devices by JAX's collectives and lax.ppermute only.
A program may use at most 64 MiB of HBM per device.

```python
import jax
import jax.numpy as jnp

NMU = 2
CX = 8
CY = 8
CZ = 128
BZ = 16
RUN = 4
STEPS = 4
NX = 16
NY = 32
NZ = 512
NBZ = 32
LIFT = 32
N_GX = 2
N_GY = 4


def front_starts(key):
    base = jax.random.fold_in(key, 7)
    first = jax.random.fold_in(base, 0)
    columns = NX // CX * (NY // CY)
    bricks = NZ // CZ
    per_brick = CZ // BZ
    common = bricks // 2 * per_brick
    jitter = jax.random.randint(first, (columns,), 0, per_brick)
    starts = common + jitter
    starts = starts.at[0].set(common)
    starts = starts.at[1].set(common + per_brick - 1)
    return starts.astype(jnp.int32)


def draw_front_blocks(key, part):
    starts = front_starts(key)
    gyn = NY // CY
    columns = NX // CX * gyn
    index = jnp.arange(columns * RUN, dtype=jnp.int32)
    column = index // RUN
    within = index % RUN
    rows = jnp.stack([column // gyn, column % gyn, starts[column] + within], 1).astype(jnp.int32)
    order = jax.random.permutation(jax.random.fold_in(key, 11), columns * RUN)
    return rows[order]


def draw_labels(key, part):
    starts = front_starts(key)
    gyn = NY // CY
    xpos = jnp.arange(NX, dtype=jnp.int32)
    ypos = jnp.arange(NY, dtype=jnp.int32)
    column = (xpos // CX)[:, None] * gyn + (ypos // CY)[None, :]
    lowest = starts[column] * BZ
    height = lowest + jax.random.randint(jax.random.fold_in(key, 13), (NX, NY), BZ // 2, RUN * BZ - BZ // 2 + 1)
    solid = jax.random.randint(jax.random.fold_in(key, 17), (NX, NY, NZ), 1, 4)
    zpos = jnp.arange(NZ, dtype=jnp.int32)
    return jnp.where(zpos[None, None, :] < height[:, :, None], solid, 0).astype(jnp.int32)


def block_levels(stream_key, dims, cuts, low, top_value):
    gain = 1.0
    for axis_at, blocks in cuts:
        steps = jax.random.uniform(jax.random.fold_in(jax.random.fold_in(stream_key, 6), axis_at), (blocks,), jnp.float32, low / len(cuts), top_value / len(cuts))
        gain = gain * jnp.repeat(jnp.exp(steps), dims[axis_at] // blocks).reshape((-1,) + (1,) * (len(dims) - 1 - axis_at))
    return gain


def centred(key, shape, scale, most, cuts=(), kind=jnp.bfloat16):
    values = jax.random.normal(key, shape, jnp.float32) * scale
    if len(cuts) > 0:
        values = block_levels(key, shape, cuts, -0.22, 0.18) * values
    return jnp.clip(values, min=-most, max=most).astype(kind)


def setup_inputs(seed: int = 0) -> dict:
    key_of = jax.random.split(jax.random.key(seed), 4)
    labels = draw_labels(jax.random.fold_in(key_of[3], 71), 0)
    mu_start = centred(key_of[1], (NMU, NX, NY, NZ), 0.5, 4.0, ((1, 2), (2, 4), (3, 4)), jnp.float32)
    front_blocks = draw_front_blocks(jax.random.fold_in(key_of[3], 71), 0)
    return {"labels": labels, "mu_start": mu_start, "front_blocks": front_blocks}


COMP = ((0.0, 0.0), (1.0, -0.5), (-0.5, 1.0), (-0.5, -0.5))
LATENT = (0.0, 1.0, 1.0, 1.0)
DT = 0.05
KAPPA = 1.5
WELL = 12.0
DLIQ = 3.0
DSOL = 0.3


def neighbours(padded):
    return [padded[..., 2:, 1:-1, 1:-1], padded[..., :-2, 1:-1, 1:-1],
            padded[..., 1:-1, 2:, 1:-1], padded[..., 1:-1, :-2, 1:-1],
            padded[..., 1:-1, 1:-1, 2:], padded[..., 1:-1, 1:-1, :-2]]


def phase_update(padded, zglob, offset, depth):
    centre = padded[:, 1:-1, 1:-1, 1:-1]
    phi = centre[:4]
    chem = centre[4:]
    beside_all = neighbours(padded[:4])
    total = beside_all[0] + beside_all[1] + beside_all[2] + beside_all[3] + beside_all[4] + beside_all[5]
    lap = total - 6.0 * phi
    square = phi * phi
    summed = square[0] + square[1] + square[2] + square[3]
    under = 2.0 * ((zglob + offset).astype(jnp.float32) / depth - 0.5)
    rates = []
    for phase in range(4):
        psi = -(COMP[phase][0] * chem[0] + COMP[phase][1] * chem[1]) + LATENT[phase] * under
        rate = KAPPA * lap[phase] - WELL * phi[phase] * (summed - square[phase]) - 6.0 * phi[phase] * (1.0 - phi[phase]) * psi
        rates.append(rate)
    mean_rate = (rates[0] + rates[1] + rates[2] + rates[3]) * 0.25
    return jnp.stack([phi[phase] + DT * (rates[phase] - mean_rate) for phase in range(4)])


def shape_fn(values):
    return values * values * (3.0 - 2.0 * values)


def chem_update(padded, phi_old, phi_new):
    chem = padded[4:, 1:-1, 1:-1, 1:-1]
    diffuse = DSOL + (DLIQ - DSOL) * padded[0]
    centre_d = diffuse[1:-1, 1:-1, 1:-1]
    side_d = neighbours(diffuse)
    side_m = neighbours(padded[4:])
    flux = jnp.zeros_like(chem)
    for way in range(6):
        flux = flux + 0.5 * (centre_d + side_d[way]) * (side_m[way] - chem)
    delta = shape_fn(phi_new) - shape_fn(phi_old)
    result = []
    for comp in range(2):
        change = COMP[0][comp] * delta[0] + COMP[1][comp] * delta[1] + COMP[2][comp] * delta[2] + COMP[3][comp] * delta[3]
        result.append(chem[comp] + DT * flux[comp] - change)
    return jnp.stack(result)


def pad_field(fields):
    fields = jnp.pad(fields, ((0, 0), (1, 1), (1, 1), (0, 0)), mode="wrap")
    return jnp.pad(fields, ((0, 0), (0, 0), (0, 0), (1, 1)), mode="edge")


def liquid(count):
    ones = jnp.ones((1, NX, NY, count), jnp.float32)
    return jnp.concatenate([ones, jnp.zeros((5, NX, NY, count), jnp.float32)], 0)


def reference(labels, mu_start, front_blocks):
    phi = jnp.stack([(labels == phase).astype(jnp.float32) for phase in range(4)])
    fields = jnp.concatenate([phi, mu_start], 0)
    marks = jnp.zeros((N_GX, N_GY, NBZ), jnp.int32).at[front_blocks[:, 0], front_blocks[:, 1], front_blocks[:, 2]].set(1)
    marks = jnp.repeat(jnp.repeat(jnp.repeat(marks, CX, 0), CY, 1), BZ, 2) > 0
    zglob = jnp.arange(NZ, dtype=jnp.int32)
    offset = 0
    for step in range(STEPS):
        if step == STEPS // 2:
            fields = jnp.concatenate([fields[..., LIFT:], liquid(LIFT)], 3)
            offset = LIFT
        padded = pad_field(fields)
        phi_new = jnp.where(marks[None], phase_update(padded, zglob, offset, NZ), fields[:4])
        mu_new = chem_update(padded, fields[:4], phi_new)
        fields = jnp.concatenate([phi_new, mu_new], 0)
    return fields[:4], fields[4:]
```

```python
import jax
import jax.numpy as jnp
from jax import lax
from jax.sharding import PartitionSpec as P

BZ = 16
STEPS = 4


COMP = ((0.0, 0.0), (1.0, -0.5), (-0.5, 1.0), (-0.5, -0.5))
LATENT = (0.0, 1.0, 1.0, 1.0)
DT = 0.05
KAPPA = 1.5
WELL = 12.0
DLIQ = 3.0
DSOL = 0.3


def ring(axis, by):
    count = lax.axis_size(axis)
    return [(i, (i + by) % count) for i in range(count)]


def line(axis, by):
    count = lax.axis_size(axis)
    return [(i, i + by) for i in range(count) if 0 <= i + by < count]


def flat_z(face):
    return face.reshape(face.shape[0], -1)


def lateral_halos(block):
    xlo = lax.ppermute(block[:, -1], "gx", ring("gx", 1))
    xhi = lax.ppermute(block[:, 0], "gx", ring("gx", -1))
    ylo = lax.ppermute(block[:, :, -1], "gy", ring("gy", 1))
    yhi = lax.ppermute(block[:, :, 0], "gy", ring("gy", -1))
    return xlo, xhi, ylo, yhi


def neighbours(fields, halos):
    xlo, xhi, ylo, yhi, zlo, zhi = halos
    return [
        jnp.concatenate([fields[:, 1:], xhi[:, None]], 1),
        jnp.concatenate([xlo[:, None], fields[:, :-1]], 1),
        jnp.concatenate([fields[:, :, 1:], yhi[:, :, None]], 2),
        jnp.concatenate([ylo[:, :, None], fields[:, :, :-1]], 2),
        jnp.concatenate([fields[..., 1:], zhi[..., None]], 3),
        jnp.concatenate([zlo[..., None], fields[..., :-1]], 3),
    ]


def phase_update(fields, side, zglob, offset, depth):
    phi = fields[:4]
    chem = fields[4:]
    beside_all = [s[:4] for s in side]
    total = (
        beside_all[0]
        + beside_all[1]
        + beside_all[2]
        + beside_all[3]
        + beside_all[4]
        + beside_all[5]
    )
    lap = total - 6.0 * phi
    square = phi * phi
    summed = square[0] + square[1] + square[2] + square[3]
    under = 2.0 * ((zglob + offset).astype(jnp.float32) / depth - 0.5)
    rates = []
    for phase in range(4):
        psi = -(COMP[phase][0] * chem[0] + COMP[phase][1] * chem[1]) + LATENT[phase] * under
        rate = (
            KAPPA * lap[phase]
            - WELL * phi[phase] * (summed - square[phase])
            - 6.0 * phi[phase] * (1.0 - phi[phase]) * psi
        )
        rates.append(rate)
    mean_rate = (rates[0] + rates[1] + rates[2] + rates[3]) * 0.25
    return jnp.stack([phi[phase] + DT * (rates[phase] - mean_rate) for phase in range(4)])


def shape_fn(values):
    return values * values * (3.0 - 2.0 * values)


def chem_update(fields, side, phi_old, phi_new):
    chem = fields[4:]
    centre_d = DSOL + (DLIQ - DSOL) * fields[0]
    side_d = [DSOL + (DLIQ - DSOL) * s[0] for s in side]
    side_m = [s[4:] for s in side]
    flux = jnp.zeros_like(chem)
    for way in range(6):
        flux = flux + 0.5 * (centre_d + side_d[way]) * (side_m[way] - chem)
    delta = shape_fn(phi_new) - shape_fn(phi_old)
    result = []
    for comp in range(2):
        change = (
            COMP[0][comp] * delta[0]
            + COMP[1][comp] * delta[1]
            + COMP[2][comp] * delta[2]
            + COMP[3][comp] * delta[3]
        )
        result.append(chem[comp] + DT * flux[comp] - change)
    return jnp.stack(result)


def shards(labels, mu_start, front_blocks):
    cells_x, cells_y, cells_z = labels.shape
    lift = cells_z // 4
    bricks_z = lax.axis_size("gz")
    depth = cells_z * bricks_z
    index_x = lax.axis_index("gx")
    index_y = lax.axis_index("gy")
    index_z = lax.axis_index("gz")
    zglob = index_z * cells_z + jnp.arange(cells_z, dtype=jnp.int32)
    per_brick = cells_z // BZ
    bottom_brick = index_z == 0
    top_brick = index_z == bricks_z - 1

    matched = (
        (front_blocks[:, 0] == index_x)
        & (front_blocks[:, 1] == index_y)
        & (front_blocks[:, 2] // per_brick == index_z)
    )
    local_block = front_blocks[:, 2] - index_z * per_brick
    hits = matched[:, None] & (
        local_block[:, None] == jnp.arange(per_brick, dtype=jnp.int32)[None, :]
    )
    block_on = jnp.any(hits, 0)
    cell_on = jnp.repeat(block_on, BZ)

    phi_start = jnp.stack([(labels == phase).astype(jnp.float32) for phase in range(4)])
    fields = jnp.concatenate([phi_start, mu_start], 0)
    nf = fields.shape[0]
    offset = 0
    for step in range(STEPS):
        if step == STEPS // 2:
            offset = lift
            incoming = lax.ppermute(fields[..., : lift + 1], "gz", line("gz", -1))
            count = lift + 1
            ones = jnp.ones((1, cells_x, cells_y, count), jnp.float32)
            incoming = jnp.where(
                top_brick,
                jnp.concatenate([ones, jnp.zeros((nf - 1, cells_x, cells_y, count), jnp.float32)], 0),
                incoming,
            )
            zlo = jnp.where(bottom_brick, fields[..., lift], fields[..., lift - 1])
            fields = jnp.concatenate([fields[..., lift:], incoming[..., :lift]], 3)
            zhi = incoming[..., lift]
            xlo, xhi, ylo, yhi = lateral_halos(fields)
        else:
            xlo, xhi, ylo, yhi = lateral_halos(fields)
            from_below = lax.ppermute(flat_z(fields[..., -1]), "gz", line("gz", 1))
            from_above = lax.ppermute(flat_z(fields[..., 0]), "gz", line("gz", -1))
            zlo = jnp.where(bottom_brick, fields[..., 0], from_below.reshape(fields.shape[:3]))
            zhi = jnp.where(top_brick, fields[..., -1], from_above.reshape(fields.shape[:3]))
        side = neighbours(fields, (xlo, xhi, ylo, yhi, zlo, zhi))
        phi_new = jnp.where(
            cell_on[None, None, None, :],
            phase_update(fields, side, zglob, offset, depth),
            fields[:4],
        )
        mu_new = chem_update(fields, side, fields[:4], phi_new)
        fields = jnp.concatenate([phi_new, mu_new], 0)
    return (fields[:4], fields[4:])


def solution(mesh):
    placed = (P("gx", "gy", "gz"), P(None, "gx", "gy", "gz"), P())
    return jax.shard_map(
        shards,
        mesh=mesh,
        in_specs=placed,
        out_specs=(P(None, "gx", "gy", "gz"), P(None, "gx", "gy", "gz")),
        check_vma=False,
    )
```

```python
import jax
import jax.numpy as jnp
from jax import lax
from jax.sharding import PartitionSpec as P

BZ = 16


COMP = ((0.0, 0.0), (1.0, -0.5), (-0.5, 1.0), (-0.5, -0.5))
LATENT = (0.0, 1.0, 1.0, 1.0)
DT = 0.05
KAPPA = 1.5
WELL = 12.0
DLIQ = 3.0
DSOL = 0.3


def ring(axis, by):
    count = lax.axis_size(axis)
    return [(i, (i + by) % count) for i in range(count)]


def line(axis, by):
    count = lax.axis_size(axis)
    return [(i, i + by) for i in range(count) if 0 <= i + by < count]


def lateral_halos(block):
    if lax.axis_size("gx") == 2:
        pair = jnp.stack([block[:, -1], block[:, 0]])
        got = lax.ppermute(pair, "gx", ring("gx", 1))
        xlo, xhi = got[0], got[1]
    else:
        xlo = lax.ppermute(block[:, -1], "gx", ring("gx", 1))
        xhi = lax.ppermute(block[:, 0], "gx", ring("gx", -1))
    ylo = lax.ppermute(block[:, :, -1], "gy", ring("gy", 1))
    yhi = lax.ppermute(block[:, :, 0], "gy", ring("gy", -1))
    return xlo, xhi, ylo, yhi


def neighbours(fields, halos):
    xlo, xhi, ylo, yhi, zlo, zhi = halos
    return [
        jnp.concatenate([fields[:, 1:], xhi[:, None]], 1),
        jnp.concatenate([xlo[:, None], fields[:, :-1]], 1),
        jnp.concatenate([fields[:, :, 1:], yhi[:, :, None]], 2),
        jnp.concatenate([ylo[:, :, None], fields[:, :, :-1]], 2),
        jnp.concatenate([fields[..., 1:], zhi[..., None]], 3),
        jnp.concatenate([zlo[..., None], fields[..., :-1]], 3),
    ]


def phase_update(fields, side, zglob, offset, depth):
    phi = fields[:4]
    chem = fields[4:]
    beside_all = [s[:4] for s in side]
    total = (
        beside_all[0]
        + beside_all[1]
        + beside_all[2]
        + beside_all[3]
        + beside_all[4]
        + beside_all[5]
    )
    lap = total - 6.0 * phi
    square = phi * phi
    summed = square[0] + square[1] + square[2] + square[3]
    under = 2.0 * ((zglob + offset).astype(jnp.float32) / depth - 0.5)
    rates = []
    for phase in range(4):
        psi = -(COMP[phase][0] * chem[0] + COMP[phase][1] * chem[1]) + LATENT[phase] * under
        rate = (
            KAPPA * lap[phase]
            - WELL * phi[phase] * (summed - square[phase])
            - 6.0 * phi[phase] * (1.0 - phi[phase]) * psi
        )
        rates.append(rate)
    mean_rate = (rates[0] + rates[1] + rates[2] + rates[3]) * 0.25
    return jnp.stack([phi[phase] + DT * (rates[phase] - mean_rate) for phase in range(4)])


def shape_fn(values):
    return values * values * (3.0 - 2.0 * values)


def chem_update(fields, side, phi_old, phi_new):
    chem = fields[4:]
    centre_d = DSOL + (DLIQ - DSOL) * fields[0]
    side_d = [DSOL + (DLIQ - DSOL) * s[0] for s in side]
    side_m = [s[4:] for s in side]
    flux = jnp.zeros_like(chem)
    for way in range(6):
        flux = flux + 0.5 * (centre_d + side_d[way]) * (side_m[way] - chem)
    delta = shape_fn(phi_new) - shape_fn(phi_old)
    result = []
    for comp in range(2):
        change = (
            COMP[0][comp] * delta[0]
            + COMP[1][comp] * delta[1]
            + COMP[2][comp] * delta[2]
            + COMP[3][comp] * delta[3]
        )
        result.append(chem[comp] + DT * flux[comp] - change)
    return jnp.stack(result)


def shards(labels, mu_start, front_blocks):
    cells_x, cells_y, cells_z = labels.shape
    lift = cells_z // 4
    bricks_z = lax.axis_size("gz")
    depth = cells_z * bricks_z
    index_x = lax.axis_index("gx")
    index_y = lax.axis_index("gy")
    index_z = lax.axis_index("gz")
    bottom_brick = index_z == 0
    top_brick = index_z == bricks_z - 1
    zext = index_z * cells_z + jnp.arange(-1, cells_z + 1, dtype=jnp.int32)
    zown = zext[1:-1]

    matched = (front_blocks[:, 0] == index_x) & (front_blocks[:, 1] == index_y)

    def active(zpos):
        block = jnp.floor_divide(zpos, BZ)
        hits = matched[:, None] & (front_blocks[:, 2][:, None] == block[None, :])
        return jnp.any(hits, 0)

    on_ext = active(zext)
    on_own = on_ext[1:-1]

    def step(fields, zlo, zhi, zpos, cell_on, offset):
        xlo, xhi, ylo, yhi = lateral_halos(fields)
        side = neighbours(fields, (xlo, xhi, ylo, yhi, zlo, zhi))
        phi_new = jnp.where(
            cell_on[None, None, None, :],
            phase_update(fields, side, zpos, offset, depth),
            fields[:4],
        )
        mu_new = chem_update(fields, side, fields[:4], phi_new)
        return jnp.concatenate([phi_new, mu_new], 0)

    def close_ext(ext):
        low = jnp.where(bottom_brick, ext[..., 1:2], ext[..., 0:1])
        high = jnp.where(top_brick, ext[..., -2:-1], ext[..., -1:])
        return jnp.concatenate([low, ext[..., 1:-1], high], 3)

    def two_step(ext, offset):
        mid = close_ext(ext[..., 1:-1])
        first = step(mid, ext[..., 0], ext[..., -1], zext, on_ext, offset)
        first = close_ext(first)
        return step(first[..., 1:-1], first[..., 0], first[..., -1], zown, on_own, offset)

    phi_start = jnp.stack([(labels == phase).astype(jnp.float32) for phase in range(4)])
    fields = jnp.concatenate([phi_start, mu_start], 0)
    nf = fields.shape[0]
    shape_xy = fields.shape[1:3]

    def flat(part):
        return part.reshape(nf, -1)

    from_above = lax.ppermute(flat(fields[..., :2]), "gz", line("gz", -1))
    from_below = lax.ppermute(flat(fields[..., -2:]), "gz", line("gz", 1))
    ext = jnp.concatenate(
        [from_below.reshape((nf,) + shape_xy + (2,)), fields, from_above.reshape((nf,) + shape_xy + (2,))], 3
    )
    fields = two_step(ext, 0)

    count = lift + 2
    incoming = lax.ppermute(flat(fields[..., :count]), "gz", line("gz", -1))
    incoming = incoming.reshape((nf,) + shape_xy + (count,))
    ones = jnp.ones((1,) + shape_xy + (count,), jnp.float32)
    incoming = jnp.where(
        top_brick,
        jnp.concatenate([ones, jnp.zeros((nf - 1,) + shape_xy + (count,), jnp.float32)], 0),
        incoming,
    )
    ext = jnp.concatenate([fields[..., lift - 2 :], incoming], 3)
    fields = two_step(ext, lift)
    return (fields[:4], fields[4:])


def solution(mesh):
    placed = (P("gx", "gy", "gz"), P(None, "gx", "gy", "gz"), P())
    return jax.shard_map(
        shards,
        mesh=mesh,
        in_specs=placed,
        out_specs=(P(None, "gx", "gy", "gz"), P(None, "gx", "gy", "gz")),
        check_vma=False,
    )
```

```python
import jax
import jax.numpy as jnp
from jax import lax
from jax.sharding import PartitionSpec as P

BZ = 16


COMP = ((0.0, 0.0), (1.0, -0.5), (-0.5, 1.0), (-0.5, -0.5))
LATENT = (0.0, 1.0, 1.0, 1.0)
DT = 0.05
KAPPA = 1.5
WELL = 12.0
DLIQ = 3.0
DSOL = 0.3


def ring(axis, by):
    count = lax.axis_size(axis)
    return [(i, (i + by) % count) for i in range(count)]


def line(axis, by):
    count = lax.axis_size(axis)
    return [(i, i + by) for i in range(count) if 0 <= i + by < count]


def lateral_halos(block):
    if lax.axis_size("gx") == 2:
        pair = jnp.stack([block[:, -1], block[:, 0]])
        got = lax.ppermute(pair, "gx", ring("gx", 1))
        xlo, xhi = got[0], got[1]
    else:
        xlo = lax.ppermute(block[:, -1], "gx", ring("gx", 1))
        xhi = lax.ppermute(block[:, 0], "gx", ring("gx", -1))
    ylo = lax.ppermute(block[:, :, -1], "gy", ring("gy", 1))
    yhi = lax.ppermute(block[:, :, 0], "gy", ring("gy", -1))
    return xlo, xhi, ylo, yhi


def neighbours(fields, halos):
    xlo, xhi, ylo, yhi, zlo, zhi = halos
    return [
        jnp.concatenate([fields[:, 1:], xhi[:, None]], 1),
        jnp.concatenate([xlo[:, None], fields[:, :-1]], 1),
        jnp.concatenate([fields[:, :, 1:], yhi[:, :, None]], 2),
        jnp.concatenate([ylo[:, :, None], fields[:, :, :-1]], 2),
        jnp.concatenate([fields[..., 1:], zhi[..., None]], 3),
        jnp.concatenate([zlo[..., None], fields[..., :-1]], 3),
    ]


def phase_update(fields, side, zglob, offset, depth):
    phi = fields[:4]
    chem = fields[4:]
    beside_all = [s[:4] for s in side]
    total = (
        beside_all[0]
        + beside_all[1]
        + beside_all[2]
        + beside_all[3]
        + beside_all[4]
        + beside_all[5]
    )
    lap = total - 6.0 * phi
    square = phi * phi
    summed = square[0] + square[1] + square[2] + square[3]
    under = 2.0 * ((zglob + offset).astype(jnp.float32) / depth - 0.5)
    rates = []
    for phase in range(4):
        psi = -(COMP[phase][0] * chem[0] + COMP[phase][1] * chem[1]) + LATENT[phase] * under
        rate = (
            KAPPA * lap[phase]
            - WELL * phi[phase] * (summed - square[phase])
            - 6.0 * phi[phase] * (1.0 - phi[phase]) * psi
        )
        rates.append(rate)
    mean_rate = (rates[0] + rates[1] + rates[2] + rates[3]) * 0.25
    return jnp.stack([phi[phase] + DT * (rates[phase] - mean_rate) for phase in range(4)])


def shape_fn(values):
    return values * values * (3.0 - 2.0 * values)


def chem_update(fields, side, phi_old, phi_new):
    chem = fields[4:]
    centre_d = DSOL + (DLIQ - DSOL) * fields[0]
    side_d = [DSOL + (DLIQ - DSOL) * s[0] for s in side]
    side_m = [s[4:] for s in side]
    flux = jnp.zeros_like(chem)
    for way in range(6):
        flux = flux + 0.5 * (centre_d + side_d[way]) * (side_m[way] - chem)
    delta = shape_fn(phi_new) - shape_fn(phi_old)
    result = []
    for comp in range(2):
        change = (
            COMP[0][comp] * delta[0]
            + COMP[1][comp] * delta[1]
            + COMP[2][comp] * delta[2]
            + COMP[3][comp] * delta[3]
        )
        result.append(chem[comp] + DT * flux[comp] - change)
    return jnp.stack(result)


def shards(labels, mu_start, front_blocks):
    cells_x, cells_y, cells_z = labels.shape
    lift = cells_z // 4
    bricks_z = lax.axis_size("gz")
    depth = cells_z * bricks_z
    index_x = lax.axis_index("gx")
    index_y = lax.axis_index("gy")
    index_z = lax.axis_index("gz")
    bottom_brick = index_z == 0
    top_brick = index_z == bricks_z - 1
    base_z = index_z * cells_z

    matched = (front_blocks[:, 0] == index_x) & (front_blocks[:, 1] == index_y)

    def active(zpos):
        block = jnp.floor_divide(zpos, BZ)
        hits = matched[:, None] & (front_blocks[:, 2][:, None] == block[None, :])
        return jnp.any(hits, 0)

    def step(ext, first, offset):
        fields = ext[..., 1:-1]
        zpos = base_z + first + jnp.arange(fields.shape[3], dtype=jnp.int32)
        xlo, xhi, ylo, yhi = lateral_halos(fields)
        side = neighbours(fields, (xlo, xhi, ylo, yhi, ext[..., 0], ext[..., -1]))
        phi_new = jnp.where(
            active(zpos)[None, None, None, :],
            phase_update(fields, side, zpos, offset, depth),
            fields[:4],
        )
        mu_new = chem_update(fields, side, fields[:4], phi_new)
        return jnp.concatenate([phi_new, mu_new], 0)

    def layer_index(ext):
        return lax.broadcasted_iota(jnp.int32, ext.shape, 3)

    def edge_at(ext, at, cond):
        up = jnp.concatenate([ext[..., :1], ext[..., :-1]], 3)
        return jnp.where(cond & (layer_index(ext) == at), up, ext)

    def edge_below(ext, at, cond):
        down = jnp.concatenate([ext[..., 1:], ext[..., -1:]], 3)
        return jnp.where(cond & (layer_index(ext) == at), down, ext)

    phi_start = jnp.stack([(labels == phase).astype(jnp.float32) for phase in range(4)])
    fields = jnp.concatenate([phi_start, mu_start], 0)
    nf = fields.shape[0]
    shape_xy = fields.shape[1:3]

    low = lift - 4
    count = lift + 4
    above = lax.ppermute(fields[..., :count].reshape(nf, -1), "gz", line("gz", -1))
    ext = jnp.concatenate([fields[..., low:], above.reshape((nf,) + shape_xy + (count,))], 3)
    ext = edge_at(ext, cells_z - low, top_brick)
    ext = step(ext, low + 1, 0)
    ext = edge_at(ext, cells_z - low - 1, top_brick)
    ext = step(ext, low + 2, 0)
    liquid = jnp.concatenate(
        [jnp.ones((1,) + ext.shape[1:], jnp.float32), jnp.zeros((nf - 1,) + ext.shape[1:], jnp.float32)], 0
    )
    ext = jnp.where(top_brick & (layer_index(ext) >= cells_z - lift + 2), liquid, ext)
    ext = edge_below(ext, 1, bottom_brick)
    ext = edge_at(ext, cells_z + 2, top_brick)
    ext = step(ext, -1, lift)
    ext = edge_below(ext, 0, bottom_brick)
    ext = edge_at(ext, cells_z + 1, top_brick)
    fields = step(ext, 0, lift)
    return (fields[:4], fields[4:])


def solution(mesh):
    placed = (P("gx", "gy", "gz"), P(None, "gx", "gy", "gz"), P())
    return jax.shard_map(
        shards,
        mesh=mesh,
        in_specs=placed,
        out_specs=(P(None, "gx", "gy", "gz"), P(None, "gx", "gy", "gz")),
        check_vma=False,
    )
```

```python
import jax
import jax.numpy as jnp
from jax import lax
from jax.sharding import PartitionSpec as P

BZ = 16


COMP = ((0.0, 0.0), (1.0, -0.5), (-0.5, 1.0), (-0.5, -0.5))
LATENT = (0.0, 1.0, 1.0, 1.0)
DT = 0.05
KAPPA = 1.5
WELL = 12.0
DLIQ = 3.0
DSOL = 0.3


def ring(axis, by):
    count = lax.axis_size(axis)
    return [(i, (i + by) % count) for i in range(count)]


def line(axis, by):
    count = lax.axis_size(axis)
    return [(i, i + by) for i in range(count) if 0 <= i + by < count]


def x_halos(block):
    if lax.axis_size("gx") == 2:
        pair = jnp.stack([block[:, -1], block[:, 0]])
        got = lax.ppermute(pair, "gx", ring("gx", 1))
        return got[0], got[1]
    xlo = lax.ppermute(block[:, -1], "gx", ring("gx", 1))
    xhi = lax.ppermute(block[:, 0], "gx", ring("gx", -1))
    return xlo, xhi


def neighbours(ext, xlo, xhi):
    fields = ext[:, :, 1:-1, 1:-1]
    return [
        jnp.concatenate([fields[:, 1:], xhi[:, None]], 1),
        jnp.concatenate([xlo[:, None], fields[:, :-1]], 1),
        ext[:, :, 2:, 1:-1],
        ext[:, :, :-2, 1:-1],
        ext[:, :, 1:-1, 2:],
        ext[:, :, 1:-1, :-2],
    ]


def phase_update(fields, side, zglob, offset, depth):
    phi = fields[:4]
    chem = fields[4:]
    beside_all = [s[:4] for s in side]
    total = (
        beside_all[0]
        + beside_all[1]
        + beside_all[2]
        + beside_all[3]
        + beside_all[4]
        + beside_all[5]
    )
    lap = total - 6.0 * phi
    square = phi * phi
    summed = square[0] + square[1] + square[2] + square[3]
    under = 2.0 * ((zglob + offset).astype(jnp.float32) / depth - 0.5)
    rates = []
    for phase in range(4):
        psi = -(COMP[phase][0] * chem[0] + COMP[phase][1] * chem[1]) + LATENT[phase] * under
        rate = (
            KAPPA * lap[phase]
            - WELL * phi[phase] * (summed - square[phase])
            - 6.0 * phi[phase] * (1.0 - phi[phase]) * psi
        )
        rates.append(rate)
    mean_rate = (rates[0] + rates[1] + rates[2] + rates[3]) * 0.25
    return jnp.stack([phi[phase] + DT * (rates[phase] - mean_rate) for phase in range(4)])


def shape_fn(values):
    return values * values * (3.0 - 2.0 * values)


def chem_update(fields, side, phi_old, phi_new):
    chem = fields[4:]
    centre_d = DSOL + (DLIQ - DSOL) * fields[0]
    side_d = [DSOL + (DLIQ - DSOL) * s[0] for s in side]
    side_m = [s[4:] for s in side]
    flux = jnp.zeros_like(chem)
    for way in range(6):
        flux = flux + 0.5 * (centre_d + side_d[way]) * (side_m[way] - chem)
    delta = shape_fn(phi_new) - shape_fn(phi_old)
    result = []
    for comp in range(2):
        change = (
            COMP[0][comp] * delta[0]
            + COMP[1][comp] * delta[1]
            + COMP[2][comp] * delta[2]
            + COMP[3][comp] * delta[3]
        )
        result.append(chem[comp] + DT * flux[comp] - change)
    return jnp.stack(result)


def shards(labels, mu_start, front_blocks):
    cells_x, cells_y, cells_z = labels.shape
    lift = cells_z // 4
    bricks_y = lax.axis_size("gy")
    bricks_z = lax.axis_size("gz")
    depth = cells_z * bricks_z
    index_x = lax.axis_index("gx")
    index_y = lax.axis_index("gy")
    index_z = lax.axis_index("gz")
    bottom_brick = index_z == 0
    top_brick = index_z == bricks_z - 1
    base_z = index_z * cells_z
    rim_y = 4

    in_column = front_blocks[:, 0] == index_x

    def active(ypos, zpos):
        brick_y = (index_y + jnp.floor_divide(ypos, cells_y)) % bricks_y
        block = jnp.floor_divide(zpos, BZ)
        hits = (
            in_column[:, None, None]
            & (front_blocks[:, 1][:, None, None] == brick_y[None, :, None])
            & (front_blocks[:, 2][:, None, None] == block[None, None, :])
        )
        return jnp.any(hits, 0)

    def step(ext, first_y, first_z, offset):
        fields = ext[:, :, 1:-1, 1:-1]
        ypos = first_y + jnp.arange(fields.shape[2], dtype=jnp.int32)
        zpos = base_z + first_z + jnp.arange(fields.shape[3], dtype=jnp.int32)
        xlo, xhi = x_halos(fields)
        side = neighbours(ext, xlo, xhi)
        phi_new = jnp.where(
            active(ypos, zpos)[None, None],
            phase_update(fields, side, zpos, offset, depth),
            fields[:4],
        )
        mu_new = chem_update(fields, side, fields[:4], phi_new)
        return jnp.concatenate([phi_new, mu_new], 0)

    def layer_index(ext):
        return lax.broadcasted_iota(jnp.int32, ext.shape, 3)

    def edge_at(ext, at, cond):
        up = jnp.concatenate([ext[..., :1], ext[..., :-1]], 3)
        return jnp.where(cond & (layer_index(ext) == at), up, ext)

    def edge_below(ext, at, cond):
        down = jnp.concatenate([ext[..., 1:], ext[..., -1:]], 3)
        return jnp.where(cond & (layer_index(ext) == at), down, ext)

    phi_start = jnp.stack([(labels == phase).astype(jnp.float32) for phase in range(4)])
    fields = jnp.concatenate([phi_start, mu_start], 0)
    nf = fields.shape[0]
    shape_xy = fields.shape[1:3]

    low = lift - 4
    count = lift + 4
    above = lax.ppermute(fields[..., :count].reshape(nf, -1), "gz", line("gz", -1))
    ext = jnp.concatenate([fields[..., low:], above.reshape((nf,) + shape_xy + (count,))], 3)
    below_y = lax.ppermute(ext[:, :, -rim_y:], "gy", ring("gy", 1))
    above_y = lax.ppermute(ext[:, :, :rim_y], "gy", ring("gy", -1))
    ext = jnp.concatenate([below_y, ext, above_y], 2)
    ext = edge_at(ext, cells_z - low, top_brick)
    ext = step(ext, 1 - rim_y, low + 1, 0)
    ext = edge_at(ext, cells_z - low - 1, top_brick)
    ext = step(ext, 2 - rim_y, low + 2, 0)
    liquid = jnp.concatenate(
        [jnp.ones((1,) + ext.shape[1:], jnp.float32), jnp.zeros((nf - 1,) + ext.shape[1:], jnp.float32)], 0
    )
    ext = jnp.where(top_brick & (layer_index(ext) >= cells_z - lift + 2), liquid, ext)
    ext = edge_below(ext, 1, bottom_brick)
    ext = edge_at(ext, cells_z + 2, top_brick)
    ext = step(ext, 3 - rim_y, -1, lift)
    ext = edge_below(ext, 0, bottom_brick)
    ext = edge_at(ext, cells_z + 1, top_brick)
    fields = step(ext, 4 - rim_y, 0, lift)
    return (fields[:4], fields[4:])


def solution(mesh):
    placed = (P("gx", "gy", "gz"), P(None, "gx", "gy", "gz"), P())
    return jax.shard_map(
        shards,
        mesh=mesh,
        in_specs=placed,
        out_specs=(P(None, "gx", "gy", "gz"), P(None, "gx", "gy", "gz")),
        check_vma=False,
    )
```

```python
import jax
import jax.numpy as jnp
from jax import lax
from jax.sharding import PartitionSpec as P

BZ = 16


COMP = ((0.0, 0.0), (1.0, -0.5), (-0.5, 1.0), (-0.5, -0.5))
LATENT = (0.0, 1.0, 1.0, 1.0)
DT = 0.05
KAPPA = 1.5
WELL = 12.0
DLIQ = 3.0
DSOL = 0.3


def ring(axis, by):
    count = lax.axis_size(axis)
    return [(i, (i + by) % count) for i in range(count)]


def line(axis, by):
    count = lax.axis_size(axis)
    return [(i, i + by) for i in range(count) if 0 <= i + by < count]


def x_halos(block):
    if lax.axis_size("gx") == 2:
        pair = jnp.stack([block[:, -1], block[:, 0]])
        got = lax.ppermute(pair, "gx", ring("gx", 1))
        return got[0], got[1]
    xlo = lax.ppermute(block[:, -1], "gx", ring("gx", 1))
    xhi = lax.ppermute(block[:, 0], "gx", ring("gx", -1))
    return xlo, xhi


def neighbours(ext, xlo, xhi):
    fields = ext[:, :, 1:-1, 1:-1]
    return [
        jnp.concatenate([fields[:, 1:], xhi[:, None]], 1),
        jnp.concatenate([xlo[:, None], fields[:, :-1]], 1),
        ext[:, :, 2:, 1:-1],
        ext[:, :, :-2, 1:-1],
        ext[:, :, 1:-1, 2:],
        ext[:, :, 1:-1, :-2],
    ]


def phase_update(fields, side, zglob, offset, depth):
    phi = fields[:4]
    chem = fields[4:]
    beside_all = [s[:4] for s in side]
    total = (
        beside_all[0]
        + beside_all[1]
        + beside_all[2]
        + beside_all[3]
        + beside_all[4]
        + beside_all[5]
    )
    lap = total - 6.0 * phi
    square = phi * phi
    summed = square[0] + square[1] + square[2] + square[3]
    under = 2.0 * ((zglob + offset).astype(jnp.float32) / depth - 0.5)
    rates = []
    for phase in range(4):
        psi = -(COMP[phase][0] * chem[0] + COMP[phase][1] * chem[1]) + LATENT[phase] * under
        rate = (
            KAPPA * lap[phase]
            - WELL * phi[phase] * (summed - square[phase])
            - 6.0 * phi[phase] * (1.0 - phi[phase]) * psi
        )
        rates.append(rate)
    mean_rate = (rates[0] + rates[1] + rates[2] + rates[3]) * 0.25
    return jnp.stack([phi[phase] + DT * (rates[phase] - mean_rate) for phase in range(4)])


def shape_fn(values):
    return values * values * (3.0 - 2.0 * values)


def chem_update(fields, side, phi_old, phi_new):
    chem = fields[4:]
    centre_d = DSOL + (DLIQ - DSOL) * fields[0]
    side_d = [DSOL + (DLIQ - DSOL) * s[0] for s in side]
    side_m = [s[4:] for s in side]
    flux = jnp.zeros_like(chem)
    for way in range(6):
        flux = flux + 0.5 * (centre_d + side_d[way]) * (side_m[way] - chem)
    delta = shape_fn(phi_new) - shape_fn(phi_old)
    result = []
    for comp in range(2):
        change = (
            COMP[0][comp] * delta[0]
            + COMP[1][comp] * delta[1]
            + COMP[2][comp] * delta[2]
            + COMP[3][comp] * delta[3]
        )
        result.append(chem[comp] + DT * flux[comp] - change)
    return jnp.stack(result)


def shards(labels, mu_start, front_blocks):
    cells_x, cells_y, cells_z = labels.shape
    lift = cells_z // 4
    bricks_y = lax.axis_size("gy")
    bricks_z = lax.axis_size("gz")
    depth = cells_z * bricks_z
    index_x = lax.axis_index("gx")
    index_y = lax.axis_index("gy")
    index_z = lax.axis_index("gz")
    bottom_brick = index_z == 0
    top_brick = index_z == bricks_z - 1
    base_z = index_z * cells_z
    rim_y = 4

    in_column = front_blocks[:, 0] == index_x

    def active(ypos, zpos):
        brick_y = (index_y + jnp.floor_divide(ypos, cells_y)) % bricks_y
        block = jnp.floor_divide(zpos, BZ)
        hits = (
            in_column[:, None, None]
            & (front_blocks[:, 1][:, None, None] == brick_y[None, :, None])
            & (front_blocks[:, 2][:, None, None] == block[None, None, :])
        )
        return jnp.any(hits, 0)

    def step(ext, first_y, first_z, offset):
        fields = ext[:, :, 1:-1, 1:-1]
        ypos = first_y + jnp.arange(fields.shape[2], dtype=jnp.int32)
        zpos = base_z + first_z + jnp.arange(fields.shape[3], dtype=jnp.int32)
        xlo, xhi = x_halos(fields)
        side = neighbours(ext, xlo, xhi)
        phi_new = jnp.where(
            active(ypos, zpos)[None, None],
            phase_update(fields, side, zpos, offset, depth),
            fields[:4],
        )
        mu_new = chem_update(fields, side, fields[:4], phi_new)
        return jnp.concatenate([phi_new, mu_new], 0)

    def layer_index(ext):
        return lax.broadcasted_iota(jnp.int32, ext.shape, 3)

    def edge_at(ext, at, cond):
        up = jnp.concatenate([ext[..., :1], ext[..., :-1]], 3)
        return jnp.where(cond & (layer_index(ext) == at), up, ext)

    def edge_below(ext, at, cond):
        down = jnp.concatenate([ext[..., 1:], ext[..., -1:]], 3)
        return jnp.where(cond & (layer_index(ext) == at), down, ext)

    start = jnp.concatenate([labels.astype(jnp.float32)[None], mu_start], 0)
    nf = 4 + mu_start.shape[0]
    below_y = lax.ppermute(start[:, :, -rim_y:], "gy", ring("gy", 1))
    above_y = lax.ppermute(start[:, :, :rim_y], "gy", ring("gy", -1))
    wide = jnp.concatenate([below_y, start, above_y], 2)

    low = lift - 4
    count = lift + 4
    above = lax.ppermute(wide[..., :count].reshape(wide.shape[0], -1), "gz", line("gz", -1))
    ext = jnp.concatenate([wide[..., low:], above.reshape(wide.shape[:3] + (count,))], 3)
    ext = jnp.concatenate(
        [jnp.stack([(ext[0] == phase).astype(jnp.float32) for phase in range(4)]), ext[1:]], 0
    )
    ext = edge_at(ext, cells_z - low, top_brick)
    ext = step(ext, 1 - rim_y, low + 1, 0)
    ext = edge_at(ext, cells_z - low - 1, top_brick)
    ext = step(ext, 2 - rim_y, low + 2, 0)
    liquid = jnp.concatenate(
        [jnp.ones((1,) + ext.shape[1:], jnp.float32), jnp.zeros((nf - 1,) + ext.shape[1:], jnp.float32)], 0
    )
    ext = jnp.where(top_brick & (layer_index(ext) >= cells_z - lift + 2), liquid, ext)
    ext = edge_below(ext, 1, bottom_brick)
    ext = edge_at(ext, cells_z + 2, top_brick)
    ext = step(ext, 3 - rim_y, -1, lift)
    ext = edge_below(ext, 0, bottom_brick)
    ext = edge_at(ext, cells_z + 1, top_brick)
    fields = step(ext, 4 - rim_y, 0, lift)
    return (fields[:4], fields[4:])


def solution(mesh):
    placed = (P("gx", "gy", "gz"), P(None, "gx", "gy", "gz"), P())
    return jax.shard_map(
        shards,
        mesh=mesh,
        in_specs=placed,
        out_specs=(P(None, "gx", "gy", "gz"), P(None, "gx", "gy", "gz")),
        check_vma=False,
    )
```

```python
import jax
import jax.numpy as jnp
from jax import lax
from jax.sharding import PartitionSpec as P
from jax.experimental import pallas as pl
from jax.experimental.pallas import tpu as pltpu

BZ = 16
INTERPRET = False


COMP = ((0.0, 0.0), (1.0, -0.5), (-0.5, 1.0), (-0.5, -0.5))
LATENT = (0.0, 1.0, 1.0, 1.0)
DT = 0.05
KAPPA = 1.5
WELL = 12.0
DLIQ = 3.0
DSOL = 0.3


def ring(axis, by):
    count = lax.axis_size(axis)
    return [(i, (i + by) % count) for i in range(count)]


def line(axis, by):
    count = lax.axis_size(axis)
    return [(i, i + by) for i in range(count) if 0 <= i + by < count]


def x_halos(block):
    if lax.axis_size("gx") == 2:
        pair = jnp.stack([block[:, -1], block[:, 0]])
        got = lax.ppermute(pair, "gx", ring("gx", 1))
        return got[0], got[1]
    xlo = lax.ppermute(block[:, -1], "gx", ring("gx", 1))
    xhi = lax.ppermute(block[:, 0], "gx", ring("gx", -1))
    return xlo, xhi


def neighbours(ext, xlo, xhi):
    fields = ext[:, :, 1:-1, 1:-1]
    return [
        jnp.concatenate([fields[:, 1:], xhi[:, None]], 1),
        jnp.concatenate([xlo[:, None], fields[:, :-1]], 1),
        ext[:, :, 2:, 1:-1],
        ext[:, :, :-2, 1:-1],
        ext[:, :, 1:-1, 2:],
        ext[:, :, 1:-1, :-2],
    ]


def phase_update(fields, side, zglob, offset, depth):
    phi = fields[:4]
    chem = fields[4:]
    beside_all = [s[:4] for s in side]
    total = (
        beside_all[0]
        + beside_all[1]
        + beside_all[2]
        + beside_all[3]
        + beside_all[4]
        + beside_all[5]
    )
    lap = total - 6.0 * phi
    square = phi * phi
    summed = square[0] + square[1] + square[2] + square[3]
    under = 2.0 * ((zglob + offset).astype(jnp.float32) / depth - 0.5)
    rates = []
    for phase in range(4):
        psi = -(COMP[phase][0] * chem[0] + COMP[phase][1] * chem[1]) + LATENT[phase] * under
        rate = (
            KAPPA * lap[phase]
            - WELL * phi[phase] * (summed - square[phase])
            - 6.0 * phi[phase] * (1.0 - phi[phase]) * psi
        )
        rates.append(rate)
    mean_rate = (rates[0] + rates[1] + rates[2] + rates[3]) * 0.25
    return jnp.stack([phi[phase] + DT * (rates[phase] - mean_rate) for phase in range(4)])


def shape_fn(values):
    return values * values * (3.0 - 2.0 * values)


def chem_update(fields, side, phi_old, phi_new):
    chem = fields[4:]
    centre_d = DSOL + (DLIQ - DSOL) * fields[0]
    side_d = [DSOL + (DLIQ - DSOL) * s[0] for s in side]
    side_m = [s[4:] for s in side]
    flux = jnp.zeros_like(chem)
    for way in range(6):
        flux = flux + 0.5 * (centre_d + side_d[way]) * (side_m[way] - chem)
    delta = shape_fn(phi_new) - shape_fn(phi_old)
    result = []
    for comp in range(2):
        change = (
            COMP[0][comp] * delta[0]
            + COMP[1][comp] * delta[1]
            + COMP[2][comp] * delta[2]
            + COMP[3][comp] * delta[3]
        )
        result.append(chem[comp] + DT * flux[comp] - change)
    return jnp.stack(result)


def roll_both(value, axis):
    size = value.shape[axis]
    return pltpu.roll(value, 1, axis), pltpu.roll(value, size - 1, axis)


def step_kernel(frame_ref, halo_ref, mask_ref, under_ref, fix_ref, out_ref):
    nx = frame_ref.shape[0]
    mask = mask_ref[...] > 0.5
    under = under_ref[...]
    fix = fix_ref[...]
    lane = lax.broadcasted_iota(jnp.int32, mask.shape, 1)
    size = mask.shape[1]
    rolled = pltpu.roll(lane, 1, 1)
    forward = rolled == jnp.where(lane == 0, size - 1, lane - 1)
    take_lower = fix[0:1] > 0.5
    take_upper = fix[1:2] > 0.5
    make_liquid = fix[2:3] > 0.5

    def body(x, carry):
        fields = frame_ref[x]
        below = frame_ref[jnp.maximum(x - 1, 0)]
        beyond = frame_ref[jnp.minimum(x + 1, nx - 1)]
        xm = jnp.where(x == 0, halo_ref[0], below)
        xp = jnp.where(x == nx - 1, halo_ref[1], beyond)
        ya, yb = roll_both(fields, 1)
        za, zb = roll_both(fields, 2)
        side = [xp, xm, ya, yb, za, zb]
        phi = fields[:4]
        chem = fields[4:]
        beside_all = [s[:4] for s in side]
        total = (
            beside_all[0]
            + beside_all[1]
            + beside_all[2]
            + beside_all[3]
            + beside_all[4]
            + beside_all[5]
        )
        lap = total - 6.0 * phi
        square = phi * phi
        summed = square[0] + square[1] + square[2] + square[3]
        rates = []
        for phase in range(4):
            psi = -(COMP[phase][0] * chem[0] + COMP[phase][1] * chem[1]) + LATENT[phase] * under
            rate = (
                KAPPA * lap[phase]
                - WELL * phi[phase] * (summed - square[phase])
                - 6.0 * phi[phase] * (1.0 - phi[phase]) * psi
            )
            rates.append(rate)
        mean_rate = (rates[0] + rates[1] + rates[2] + rates[3]) * 0.25
        phi_new = jnp.stack(
            [jnp.where(mask, phi[phase] + DT * (rates[phase] - mean_rate), phi[phase]) for phase in range(4)]
        )
        centre_d = DSOL + (DLIQ - DSOL) * phi[0]
        side_d = [DSOL + (DLIQ - DSOL) * s[0] for s in side]
        side_m = [s[4:] for s in side]
        flux = jnp.zeros_like(chem)
        for way in range(6):
            flux = flux + 0.5 * (centre_d + side_d[way]) * (side_m[way] - chem)
        delta = shape_fn(phi_new) - shape_fn(phi)
        result = [phi_new[phase] for phase in range(4)]
        for comp in range(2):
            change = (
                COMP[0][comp] * delta[0]
                + COMP[1][comp] * delta[1]
                + COMP[2][comp] * delta[2]
                + COMP[3][comp] * delta[3]
            )
            result.append(chem[comp] + DT * flux[comp] - change)
        new = jnp.stack(result)
        liquid = jnp.where(lax.broadcasted_iota(jnp.int32, new.shape, 0) == 0, 1.0, 0.0)
        new = jnp.where(make_liquid, liquid, new)
        ra, rb = roll_both(new, 2)
        lower = jnp.where(forward, ra, rb)
        upper = jnp.where(forward, rb, ra)
        new = jnp.where(take_upper, upper, new)
        new = jnp.where(take_lower, lower, new)
        out_ref[x] = new
        return carry

    lax.fori_loop(0, nx, body, 0)


def run_step(frame, halo, mask, under, fix):
    return pl.pallas_call(
        step_kernel,
        out_shape=jax.ShapeDtypeStruct(frame.shape, frame.dtype),
        interpret=INTERPRET,
    )(frame, halo, mask, under, fix)


def frame_halos(frame):
    if lax.axis_size("gx") == 2:
        pair = jnp.stack([frame[-1], frame[0]])
        return lax.ppermute(pair, "gx", ring("gx", 1))
    xlo = lax.ppermute(frame[-1], "gx", ring("gx", 1))
    xhi = lax.ppermute(frame[0], "gx", ring("gx", -1))
    return jnp.stack([xlo, xhi])


def shards(labels, mu_start, front_blocks):
    cells_x, cells_y, cells_z = labels.shape
    lift = cells_z // 4
    bricks_y = lax.axis_size("gy")
    bricks_z = lax.axis_size("gz")
    depth = cells_z * bricks_z
    index_x = lax.axis_index("gx")
    index_y = lax.axis_index("gy")
    index_z = lax.axis_index("gz")
    bottom_brick = index_z == 0
    top_brick = index_z == bricks_z - 1
    base_z = index_z * cells_z
    rim_y = 4
    rows = 2 * cells_y
    lanes = 2 * cells_z
    low = lift - 4
    count = lift + 4

    row_y = jnp.arange(rows, dtype=jnp.int32)
    row_y = jnp.where(row_y < cells_y + rim_y, row_y, row_y - rows)
    lane_z = jnp.arange(lanes, dtype=jnp.int32)
    lane_z = jnp.where(lane_z < lanes - 4, lane_z, lane_z - lanes)

    in_column = front_blocks[:, 0] == index_x

    def active(zpos):
        brick_y = (index_y + jnp.floor_divide(row_y, cells_y)) % bricks_y
        block = jnp.floor_divide(zpos, BZ)
        hits = (
            in_column[:, None, None]
            & (front_blocks[:, 1][:, None, None] == brick_y[None, :, None])
            & (front_blocks[:, 2][:, None, None] == block[None, None, :])
        )
        return jnp.any(hits, 0).astype(jnp.float32)

    mask_pre = active(base_z + lane_z + lift)
    mask_post = active(base_z + lane_z)
    under = 2.0 * ((base_z + lane_z + lift).astype(jnp.float32) / depth - 0.5)
    under = under[None, :]

    def lane_flag(cond, hit):
        return jnp.where(cond & hit, 1.0, 0.0).astype(jnp.float32)

    none = jnp.zeros((lanes,), jnp.float32)
    fixes = [
        jnp.stack([lane_flag(top_brick, lane_z == cells_z - lift), none, none]),
        jnp.stack([
            lane_flag(top_brick, lane_z == cells_z),
            lane_flag(bottom_brick, lane_z == -1),
            lane_flag(top_brick, lane_z >= cells_z - lift),
        ]),
        jnp.stack([lane_flag(top_brick, lane_z == cells_z), lane_flag(bottom_brick, lane_z == -1), none]),
        jnp.stack([none, none, none]),
    ]
    masks = [mask_pre, mask_pre, mask_post, mask_post]

    start = jnp.concatenate([labels.astype(jnp.float32)[None], mu_start], 0)
    nf = 4 + mu_start.shape[0]
    from_up = lax.ppermute(start[:, :, :rim_y], "gy", ring("gy", -1))
    from_down = lax.ppermute(start[:, :, -rim_y:], "gy", ring("gy", 1))
    wide = jnp.concatenate([start, from_up, from_down], 2)
    above = lax.ppermute(wide[..., :count].reshape(wide.shape[0], -1), "gz", line("gz", -1))
    above = above.reshape(wide.shape[:3] + (count,))
    gap = jnp.zeros(wide.shape[:3] + (lanes - (cells_z - lift) - count - 4,), jnp.float32)
    frame = jnp.concatenate([wide[..., lift:], above, gap, wide[..., low:lift]], 3)
    lower = jnp.concatenate([frame[..., -1:], frame[..., :-1]], 3)
    at_top = top_brick & (lax.broadcasted_iota(jnp.int32, frame.shape, 3) == cells_z - lift)
    frame = jnp.where(at_top, lower, frame)
    frame = jnp.concatenate(
        [jnp.stack([(frame[0] == phase).astype(jnp.float32) for phase in range(4)]), frame[1:]], 0
    )
    frame = jnp.transpose(frame, (1, 0, 2, 3))
    for k in range(4):
        frame = run_step(frame, frame_halos(frame), masks[k], under, fixes[k][:, None, :][:, 0])
    out = jnp.transpose(frame[:, :, :cells_y, :cells_z], (1, 0, 2, 3))
    return out[:4], out[4:]


def solution(mesh):
    placed = (P("gx", "gy", "gz"), P(None, "gx", "gy", "gz"), P())
    return jax.shard_map(
        shards,
        mesh=mesh,
        in_specs=placed,
        out_specs=(P(None, "gx", "gy", "gz"), P(None, "gx", "gy", "gz")),
        check_vma=False,
    )
```

```python
import jax
import jax.numpy as jnp
from jax import lax
from jax.sharding import PartitionSpec as P

BZ = 16


COMP = ((0.0, 0.0), (1.0, -0.5), (-0.5, 1.0), (-0.5, -0.5))
LATENT = (0.0, 1.0, 1.0, 1.0)
DT = 0.05
KAPPA = 1.5
WELL = 12.0
DLIQ = 3.0
DSOL = 0.3


def ring(axis, by):
    count = lax.axis_size(axis)
    return [(i, (i + by) % count) for i in range(count)]


def line(axis, by):
    count = lax.axis_size(axis)
    return [(i, i + by) for i in range(count) if 0 <= i + by < count]


def x_halos(block):
    if lax.axis_size("gx") == 2:
        pair = jnp.stack([block[:, -1], block[:, 0]])
        got = lax.ppermute(pair, "gx", ring("gx", 1))
        return got[0], got[1]
    xlo = lax.ppermute(block[:, -1], "gx", ring("gx", 1))
    xhi = lax.ppermute(block[:, 0], "gx", ring("gx", -1))
    return xlo, xhi


def neighbours(ext, xlo, xhi):
    fields = ext[:, :, 1:-1, 1:-1]
    return [
        jnp.concatenate([fields[:, 1:], xhi[:, None]], 1),
        jnp.concatenate([xlo[:, None], fields[:, :-1]], 1),
        ext[:, :, 2:, 1:-1],
        ext[:, :, :-2, 1:-1],
        ext[:, :, 1:-1, 2:],
        ext[:, :, 1:-1, :-2],
    ]


def phase_update(fields, side, zglob, offset, depth):
    phi = fields[:4]
    chem = fields[4:]
    beside_all = [s[:4] for s in side]
    total = (
        beside_all[0]
        + beside_all[1]
        + beside_all[2]
        + beside_all[3]
        + beside_all[4]
        + beside_all[5]
    )
    lap = total - 6.0 * phi
    square = phi * phi
    summed = square[0] + square[1] + square[2] + square[3]
    under = 2.0 * ((zglob + offset).astype(jnp.float32) / depth - 0.5)
    rates = []
    for phase in range(4):
        psi = -(COMP[phase][0] * chem[0] + COMP[phase][1] * chem[1]) + LATENT[phase] * under
        rate = (
            KAPPA * lap[phase]
            - WELL * phi[phase] * (summed - square[phase])
            - 6.0 * phi[phase] * (1.0 - phi[phase]) * psi
        )
        rates.append(rate)
    mean_rate = (rates[0] + rates[1] + rates[2] + rates[3]) * 0.25
    return jnp.stack([phi[phase] + DT * (rates[phase] - mean_rate) for phase in range(4)])


def shape_fn(values):
    return values * values * (3.0 - 2.0 * values)


def chem_update(fields, side, phi_old, phi_new):
    chem = fields[4:]
    centre_d = DSOL + (DLIQ - DSOL) * fields[0]
    side_d = [DSOL + (DLIQ - DSOL) * s[0] for s in side]
    side_m = [s[4:] for s in side]
    flux = jnp.zeros_like(chem)
    for way in range(6):
        flux = flux + 0.5 * (centre_d + side_d[way]) * (side_m[way] - chem)
    delta = shape_fn(phi_new) - shape_fn(phi_old)
    result = []
    for comp in range(2):
        change = (
            COMP[0][comp] * delta[0]
            + COMP[1][comp] * delta[1]
            + COMP[2][comp] * delta[2]
            + COMP[3][comp] * delta[3]
        )
        result.append(chem[comp] + DT * flux[comp] - change)
    return jnp.stack(result)


def shards(labels, mu_start, front_blocks):
    cells_x, cells_y, cells_z = labels.shape
    lift = cells_z // 4
    bricks_y = lax.axis_size("gy")
    bricks_z = lax.axis_size("gz")
    depth = cells_z * bricks_z
    index_x = lax.axis_index("gx")
    index_y = lax.axis_index("gy")
    index_z = lax.axis_index("gz")
    bottom_brick = index_z == 0
    top_brick = index_z == bricks_z - 1
    base_z = index_z * cells_z
    rim_y = 4

    in_column = front_blocks[:, 0] == index_x

    def active(ypos, zpos):
        brick_y = (index_y + jnp.floor_divide(ypos, cells_y)) % bricks_y
        block = jnp.floor_divide(zpos, BZ)
        hits = (
            in_column[:, None, None]
            & (front_blocks[:, 1][:, None, None] == brick_y[None, :, None])
            & (front_blocks[:, 2][:, None, None] == block[None, None, :])
        )
        return jnp.any(hits, 0)

    def update(cext, xm, xp, ypos, zpos, offset):
        fields = cext[:, :, 1:-1, 1:-1]
        side = [xp, xm, cext[:, :, 2:, 1:-1], cext[:, :, :-2, 1:-1], cext[:, :, 1:-1, 2:], cext[:, :, 1:-1, :-2]]
        phi_new = jnp.where(
            active(ypos, zpos)[None, None],
            phase_update(fields, side, zpos, offset, depth),
            fields[:4],
        )
        mu_new = chem_update(fields, side, fields[:4], phi_new)
        return jnp.concatenate([phi_new, mu_new], 0)

    def send_faces(first, last):
        if lax.axis_size("gx") == 2:
            got = lax.ppermute(jnp.stack([last, first]), "gx", ring("gx", 1))
            return got[0], got[1]
        return (
            lax.ppermute(last, "gx", ring("gx", 1)),
            lax.ppermute(first, "gx", ring("gx", -1)),
        )

    def step(ext, halo, first_y, first_z, offset, fix, last=False):
        fields = ext[:, :, 1:-1, 1:-1]
        ypos = first_y + jnp.arange(fields.shape[2], dtype=jnp.int32)
        zpos = base_z + first_z + jnp.arange(fields.shape[3], dtype=jnp.int32)
        xlo, xhi = halo
        faces = update(
            jnp.stack([ext[:, 0], ext[:, -1]], 1),
            jnp.stack([xlo, fields[:, -2]], 1),
            jnp.stack([fields[:, 1], xhi], 1),
            ypos, zpos, offset,
        )
        faces = fix(faces)
        new_halo = None
        if not last:
            inner = faces[:, :, 1:-1, 1:-1]
            new_halo = send_faces(inner[:, 0], inner[:, 1])
        middle = fix(update(ext[:, 1:-1], fields[:, :-2], fields[:, 2:], ypos, zpos, offset))
        return jnp.concatenate([faces[:, :1], middle, faces[:, 1:]], 1), new_halo

    def layer_index(ext):
        return lax.broadcasted_iota(jnp.int32, ext.shape, 3)

    def edge_at(ext, at, cond):
        up = jnp.concatenate([ext[..., :1], ext[..., :-1]], 3)
        return jnp.where(cond & (layer_index(ext) == at), up, ext)

    def edge_below(ext, at, cond):
        down = jnp.concatenate([ext[..., 1:], ext[..., -1:]], 3)
        return jnp.where(cond & (layer_index(ext) == at), down, ext)

    start = jnp.concatenate([labels.astype(jnp.float32)[None], mu_start], 0)
    nf = 4 + mu_start.shape[0]
    below_y = lax.ppermute(start[:, :, -rim_y:], "gy", ring("gy", 1))
    above_y = lax.ppermute(start[:, :, :rim_y], "gy", ring("gy", -1))
    wide = jnp.concatenate([below_y, start, above_y], 2)

    low = lift - 4
    count = lift + 4
    above = lax.ppermute(wide[..., :count].reshape(wide.shape[0], -1), "gz", line("gz", -1))
    ext = jnp.concatenate([wide[..., low:], above.reshape(wide.shape[:3] + (count,))], 3)
    ext = jnp.concatenate(
        [jnp.stack([(ext[0] == phase).astype(jnp.float32) for phase in range(4)]), ext[1:]], 0
    )
    ext = edge_at(ext, cells_z - low, top_brick)
    inner = ext[:, :, 1:-1, 1:-1]
    halo = send_faces(inner[:, 0], inner[:, -1])

    def fix0(new):
        return edge_at(new, cells_z - low - 1, top_brick)

    def fix1(new):
        liquid = jnp.concatenate(
            [jnp.ones((1,) + new.shape[1:], jnp.float32), jnp.zeros((nf - 1,) + new.shape[1:], jnp.float32)], 0
        )
        new = jnp.where(top_brick & (layer_index(new) >= cells_z - lift + 2), liquid, new)
        new = edge_below(new, 1, bottom_brick)
        return edge_at(new, cells_z + 2, top_brick)

    def fix2(new):
        new = edge_below(new, 0, bottom_brick)
        return edge_at(new, cells_z + 1, top_brick)

    def fix3(new):
        return new

    ext, halo = step(ext, halo, 1 - rim_y, low + 1, 0, fix0)
    ext, halo = step(ext, halo, 2 - rim_y, low + 2, 0, fix1)
    ext, halo = step(ext, halo, 3 - rim_y, -1, lift, fix2)
    fields, _ = step(ext, halo, 4 - rim_y, 0, lift, fix3, last=True)
    return (fields[:4], fields[4:])


def solution(mesh):
    placed = (P("gx", "gy", "gz"), P(None, "gx", "gy", "gz"), P())
    return jax.shard_map(
        shards,
        mesh=mesh,
        in_specs=placed,
        out_specs=(P(None, "gx", "gy", "gz"), P(None, "gx", "gy", "gz")),
        check_vma=False,
    )
```

```python
import jax
import jax.numpy as jnp
from jax import lax
from jax.sharding import PartitionSpec as P

BZ = 16


COMP = ((0.0, 0.0), (1.0, -0.5), (-0.5, 1.0), (-0.5, -0.5))
LATENT = (0.0, 1.0, 1.0, 1.0)
DT = 0.05
KAPPA = 1.5
WELL = 12.0
DLIQ = 3.0
DSOL = 0.3


def ring(axis, by):
    count = lax.axis_size(axis)
    return [(i, (i + by) % count) for i in range(count)]


def line(axis, by):
    count = lax.axis_size(axis)
    return [(i, i + by) for i in range(count) if 0 <= i + by < count]


def x_halos(block):
    if lax.axis_size("gx") == 2:
        pair = jnp.stack([block[:, -1], block[:, 0]])
        got = lax.ppermute(pair, "gx", ring("gx", 1))
        return got[0], got[1]
    xlo = lax.ppermute(block[:, -1], "gx", ring("gx", 1))
    xhi = lax.ppermute(block[:, 0], "gx", ring("gx", -1))
    return xlo, xhi


def neighbours(ext, xlo, xhi):
    fields = ext[:, :, 1:-1, 1:-1]
    return [
        jnp.concatenate([fields[:, 1:], xhi[:, None]], 1),
        jnp.concatenate([xlo[:, None], fields[:, :-1]], 1),
        ext[:, :, 2:, 1:-1],
        ext[:, :, :-2, 1:-1],
        ext[:, :, 1:-1, 2:],
        ext[:, :, 1:-1, :-2],
    ]


def phase_update(fields, side, zglob, offset, depth):
    phi = fields[:4]
    chem = fields[4:]
    beside_all = [s[:4] for s in side]
    total = (
        beside_all[0]
        + beside_all[1]
        + beside_all[2]
        + beside_all[3]
        + beside_all[4]
        + beside_all[5]
    )
    lap = total - 6.0 * phi
    square = phi * phi
    summed = square[0] + square[1] + square[2] + square[3]
    under = 2.0 * ((zglob + offset).astype(jnp.float32) / depth - 0.5)
    rates = []
    for phase in range(4):
        psi = -(COMP[phase][0] * chem[0] + COMP[phase][1] * chem[1]) + LATENT[phase] * under
        rate = (
            KAPPA * lap[phase]
            - WELL * phi[phase] * (summed - square[phase])
            - 6.0 * phi[phase] * (1.0 - phi[phase]) * psi
        )
        rates.append(rate)
    mean_rate = (rates[0] + rates[1] + rates[2] + rates[3]) * 0.25
    return jnp.stack([phi[phase] + DT * (rates[phase] - mean_rate) for phase in range(4)])


def shape_fn(values):
    return values * values * (3.0 - 2.0 * values)


def chem_update(fields, side, phi_old, phi_new, centre_d, side_d):
    chem = fields[4:]
    side_m = [s[4:] for s in side]
    flux = jnp.zeros_like(chem)
    for way in range(6):
        flux = flux + (centre_d + side_d[way]) * (side_m[way] - chem)
    flux = 0.5 * flux
    delta = shape_fn(phi_new) - shape_fn(phi_old)
    result = []
    for comp in range(2):
        change = (
            COMP[0][comp] * delta[0]
            + COMP[1][comp] * delta[1]
            + COMP[2][comp] * delta[2]
            + COMP[3][comp] * delta[3]
        )
        result.append(chem[comp] + DT * flux[comp] - change)
    return jnp.stack(result)


def shards(labels, mu_start, front_blocks):
    cells_x, cells_y, cells_z = labels.shape
    lift = cells_z // 4
    bricks_y = lax.axis_size("gy")
    bricks_z = lax.axis_size("gz")
    depth = cells_z * bricks_z
    index_x = lax.axis_index("gx")
    index_y = lax.axis_index("gy")
    index_z = lax.axis_index("gz")
    bottom_brick = index_z == 0
    top_brick = index_z == bricks_z - 1
    base_z = index_z * cells_z
    rim_y = 4

    in_column = front_blocks[:, 0] == index_x

    def active(ypos, zpos):
        brick_y = (index_y + jnp.floor_divide(ypos, cells_y)) % bricks_y
        block = jnp.floor_divide(zpos, BZ)
        hits = (
            in_column[:, None, None]
            & (front_blocks[:, 1][:, None, None] == brick_y[None, :, None])
            & (front_blocks[:, 2][:, None, None] == block[None, None, :])
        )
        return jnp.any(hits, 0)

    def step(ext, first_y, first_z, offset):
        fields = ext[:, :, 1:-1, 1:-1]
        ypos = first_y + jnp.arange(fields.shape[2], dtype=jnp.int32)
        zpos = base_z + first_z + jnp.arange(fields.shape[3], dtype=jnp.int32)
        xlo, xhi = x_halos(fields)
        side = neighbours(ext, xlo, xhi)
        phi_new = jnp.where(
            active(ypos, zpos)[None, None],
            phase_update(fields, side, zpos, offset, depth),
            fields[:4],
        )
        diffuse = DSOL + (DLIQ - DSOL) * ext[0:1]
        dlo = DSOL + (DLIQ - DSOL) * xlo[0:1]
        dhi = DSOL + (DLIQ - DSOL) * xhi[0:1]
        side_d = [s[0] for s in neighbours(diffuse, dlo, dhi)]
        centre_d = diffuse[0, :, 1:-1, 1:-1]
        mu_new = chem_update(fields, side, fields[:4], phi_new, centre_d, side_d)
        return jnp.concatenate([phi_new, mu_new], 0)

    def layer_index(ext):
        return lax.broadcasted_iota(jnp.int32, ext.shape, 3)

    def edge_at(ext, at, cond):
        up = jnp.concatenate([ext[..., :1], ext[..., :-1]], 3)
        return jnp.where(cond & (layer_index(ext) == at), up, ext)

    def edge_below(ext, at, cond):
        down = jnp.concatenate([ext[..., 1:], ext[..., -1:]], 3)
        return jnp.where(cond & (layer_index(ext) == at), down, ext)

    start = jnp.concatenate([labels.astype(jnp.float32)[None], mu_start], 0)
    nf = 4 + mu_start.shape[0]
    below_y = lax.ppermute(start[:, :, -rim_y:], "gy", ring("gy", 1))
    above_y = lax.ppermute(start[:, :, :rim_y], "gy", ring("gy", -1))
    wide = jnp.concatenate([below_y, start, above_y], 2)

    low = lift - 4
    count = lift + 4
    above = lax.ppermute(wide[..., :count].reshape(wide.shape[0], -1), "gz", line("gz", -1))
    ext = jnp.concatenate([wide[..., low:], above.reshape(wide.shape[:3] + (count,))], 3)
    ext = jnp.concatenate(
        [jnp.stack([(ext[0] == phase).astype(jnp.float32) for phase in range(4)]), ext[1:]], 0
    )
    ext = edge_at(ext, cells_z - low, top_brick)
    ext = step(ext, 1 - rim_y, low + 1, 0)
    ext = edge_at(ext, cells_z - low - 1, top_brick)
    ext = step(ext, 2 - rim_y, low + 2, 0)
    liquid = jnp.concatenate(
        [jnp.ones((1,) + ext.shape[1:], jnp.float32), jnp.zeros((nf - 1,) + ext.shape[1:], jnp.float32)], 0
    )
    ext = jnp.where(top_brick & (layer_index(ext) >= cells_z - lift + 2), liquid, ext)
    ext = edge_below(ext, 1, bottom_brick)
    ext = edge_at(ext, cells_z + 2, top_brick)
    ext = step(ext, 3 - rim_y, -1, lift)
    ext = edge_below(ext, 0, bottom_brick)
    ext = edge_at(ext, cells_z + 1, top_brick)
    fields = step(ext, 4 - rim_y, 0, lift)
    return (fields[:4], fields[4:])


def solution(mesh):
    placed = (P("gx", "gy", "gz"), P(None, "gx", "gy", "gz"), P())
    return jax.shard_map(
        shards,
        mesh=mesh,
        in_specs=placed,
        out_specs=(P(None, "gx", "gy", "gz"), P(None, "gx", "gy", "gz")),
        check_vma=False,
    )
```

```python
import jax
import jax.numpy as jnp
from jax import lax
from jax.sharding import PartitionSpec as P

BZ = 16


COMP = ((0.0, 0.0), (1.0, -0.5), (-0.5, 1.0), (-0.5, -0.5))
LATENT = (0.0, 1.0, 1.0, 1.0)
DT = 0.05
KAPPA = 1.5
WELL = 12.0
DLIQ = 3.0
DSOL = 0.3


def ring(axis, by):
    count = lax.axis_size(axis)
    return [(i, (i + by) % count) for i in range(count)]


def line(axis, by):
    count = lax.axis_size(axis)
    return [(i, i + by) for i in range(count) if 0 <= i + by < count]


def x_halos(block):
    if lax.axis_size("gx") == 2:
        pair = jnp.stack([block[:, -1], block[:, 0]])
        got = lax.ppermute(pair, "gx", ring("gx", 1))
        return got[0], got[1]
    xlo = lax.ppermute(block[:, -1], "gx", ring("gx", 1))
    xhi = lax.ppermute(block[:, 0], "gx", ring("gx", -1))
    return xlo, xhi


def neighbours(ext, xlo, xhi):
    fields = ext[:, :, 1:-1, 1:-1]
    return [
        jnp.concatenate([fields[:, 1:], xhi[:, None]], 1),
        jnp.concatenate([xlo[:, None], fields[:, :-1]], 1),
        ext[:, :, 2:, 1:-1],
        ext[:, :, :-2, 1:-1],
        ext[:, :, 1:-1, 2:],
        ext[:, :, 1:-1, :-2],
    ]


def phase_update(fields, side, zglob, offset, depth):
    phi = fields[:4]
    chem = fields[4:]
    beside_all = [s[:4] for s in side]
    total = (
        beside_all[0]
        + beside_all[1]
        + beside_all[2]
        + beside_all[3]
        + beside_all[4]
        + beside_all[5]
    )
    lap = total - 6.0 * phi
    square = phi * phi
    summed = square[0] + square[1] + square[2] + square[3]
    under = 2.0 * ((zglob + offset).astype(jnp.float32) / depth - 0.5)
    rates = []
    for phase in range(4):
        psi = -(COMP[phase][0] * chem[0] + COMP[phase][1] * chem[1]) + LATENT[phase] * under
        rate = (
            KAPPA * lap[phase]
            - WELL * phi[phase] * (summed - square[phase])
            - 6.0 * phi[phase] * (1.0 - phi[phase]) * psi
        )
        rates.append(rate)
    mean_rate = (rates[0] + rates[1] + rates[2] + rates[3]) * 0.25
    return jnp.stack([phi[phase] + DT * (rates[phase] - mean_rate) for phase in range(4)])


def shape_fn(values):
    return values * values * (3.0 - 2.0 * values)


def chem_update(fields, side, phi_old, phi_new):
    chem = fields[4:]
    centre_d = DSOL + (DLIQ - DSOL) * fields[0]
    side_d = [DSOL + (DLIQ - DSOL) * s[0] for s in side]
    side_m = [s[4:] for s in side]
    flux = jnp.zeros_like(chem)
    for way in range(6):
        flux = flux + 0.5 * (centre_d + side_d[way]) * (side_m[way] - chem)
    delta = shape_fn(phi_new) - shape_fn(phi_old)
    result = []
    for comp in range(2):
        change = (
            COMP[0][comp] * delta[0]
            + COMP[1][comp] * delta[1]
            + COMP[2][comp] * delta[2]
            + COMP[3][comp] * delta[3]
        )
        result.append(chem[comp] + DT * flux[comp] - change)
    return jnp.stack(result)


def shards(labels, mu_start, front_blocks):
    cells_x, cells_y, cells_z = labels.shape
    lift = cells_z // 4
    bricks_y = lax.axis_size("gy")
    bricks_z = lax.axis_size("gz")
    depth = cells_z * bricks_z
    index_x = lax.axis_index("gx")
    index_y = lax.axis_index("gy")
    index_z = lax.axis_index("gz")
    bottom_brick = index_z == 0
    top_brick = index_z == bricks_z - 1
    base_z = index_z * cells_z
    rim_y = 4

    in_column = front_blocks[:, 0] == index_x

    def active(ypos, zpos):
        brick_y = (index_y + jnp.floor_divide(ypos, cells_y)) % bricks_y
        block = jnp.floor_divide(zpos, BZ)
        hits = (
            in_column[:, None, None]
            & (front_blocks[:, 1][:, None, None] == brick_y[None, :, None])
            & (front_blocks[:, 2][:, None, None] == block[None, None, :])
        )
        return jnp.any(hits, 0)

    def step(ext, first_y, first_z, offset):
        fields = ext[:, :, 1:-1, 1:-1]
        ypos = first_y + jnp.arange(fields.shape[2], dtype=jnp.int32)
        zpos = base_z + first_z + jnp.arange(fields.shape[3], dtype=jnp.int32)
        xlo, xhi = x_halos(fields)
        side = neighbours(ext, xlo, xhi)
        phi_new = jnp.where(
            active(ypos, zpos)[None, None],
            phase_update(fields, side, zpos, offset, depth),
            fields[:4],
        )
        mu_new = chem_update(fields, side, fields[:4], phi_new)
        return jnp.concatenate([phi_new, mu_new], 0)

    def layer_index(ext):
        return lax.broadcasted_iota(jnp.int32, ext.shape, 3)

    def edge_at(ext, at, cond):
        return ext.at[..., at].set(jnp.where(cond, ext[..., at - 1], ext[..., at]))

    def edge_below(ext, at, cond):
        return ext.at[..., at].set(jnp.where(cond, ext[..., at + 1], ext[..., at]))

    start = jnp.concatenate([labels.astype(jnp.float32)[None], mu_start], 0)
    nf = 4 + mu_start.shape[0]
    below_y = lax.ppermute(start[:, :, -rim_y:], "gy", ring("gy", 1))
    above_y = lax.ppermute(start[:, :, :rim_y], "gy", ring("gy", -1))
    wide = jnp.concatenate([below_y, start, above_y], 2)

    low = lift - 4
    count = lift + 4
    above = lax.ppermute(wide[..., :count].reshape(wide.shape[0], -1), "gz", line("gz", -1))
    ext = jnp.concatenate([wide[..., low:], above.reshape(wide.shape[:3] + (count,))], 3)
    ext = jnp.concatenate(
        [jnp.stack([(ext[0] == phase).astype(jnp.float32) for phase in range(4)]), ext[1:]], 0
    )
    ext = edge_at(ext, cells_z - low, top_brick)
    ext = step(ext, 1 - rim_y, low + 1, 0)
    ext = edge_at(ext, cells_z - low - 1, top_brick)
    ext = step(ext, 2 - rim_y, low + 2, 0)
    liquid = jnp.concatenate(
        [jnp.ones((1,) + ext.shape[1:], jnp.float32), jnp.zeros((nf - 1,) + ext.shape[1:], jnp.float32)], 0
    )
    cut = cells_z - lift + 2
    ext = ext.at[..., cut:].set(jnp.where(top_brick, liquid[..., cut:], ext[..., cut:]))
    ext = edge_below(ext, 1, bottom_brick)
    ext = edge_at(ext, cells_z + 2, top_brick)
    ext = step(ext, 3 - rim_y, -1, lift)
    ext = edge_below(ext, 0, bottom_brick)
    ext = edge_at(ext, cells_z + 1, top_brick)
    fields = step(ext, 4 - rim_y, 0, lift)
    return (fields[:4], fields[4:])


def solution(mesh):
    placed = (P("gx", "gy", "gz"), P(None, "gx", "gy", "gz"), P())
    return jax.shard_map(
        shards,
        mesh=mesh,
        in_specs=placed,
        out_specs=(P(None, "gx", "gy", "gz"), P(None, "gx", "gy", "gz")),
        check_vma=False,
    )
```

```python
import jax
import jax.numpy as jnp
from jax import lax
from jax.sharding import PartitionSpec as P

BZ = 16


COMP = ((0.0, 0.0), (1.0, -0.5), (-0.5, 1.0), (-0.5, -0.5))
LATENT = (0.0, 1.0, 1.0, 1.0)
DT = 0.05
KAPPA = 1.5
WELL = 12.0
DLIQ = 3.0
DSOL = 0.3


def ring(axis, by):
    count = lax.axis_size(axis)
    return [(i, (i + by) % count) for i in range(count)]


def line(axis, by):
    count = lax.axis_size(axis)
    return [(i, i + by) for i in range(count) if 0 <= i + by < count]


def x_halos(block):
    if lax.axis_size("gx") == 2:
        pair = jnp.stack([block[:, -1], block[:, 0]])
        got = lax.ppermute(pair, "gx", ring("gx", 1))
        return got[0], got[1]
    xlo = lax.ppermute(block[:, -1], "gx", ring("gx", 1))
    xhi = lax.ppermute(block[:, 0], "gx", ring("gx", -1))
    return xlo, xhi


def neighbours(ext, xlo, xhi, stride):
    size = ext.shape[2] - 2 * stride
    fields = ext[..., stride : stride + size]
    return [
        jnp.concatenate([fields[:, 1:], xhi[:, None]], 1),
        jnp.concatenate([xlo[:, None], fields[:, :-1]], 1),
        ext[..., 2 * stride :],
        ext[..., :size],
        ext[..., stride + 1 : stride + 1 + size],
        ext[..., stride - 1 : stride - 1 + size],
    ]


def phase_update(fields, side, zglob, offset, depth):
    phi = fields[:4]
    chem = fields[4:]
    beside_all = [s[:4] for s in side]
    total = (
        beside_all[0]
        + beside_all[1]
        + beside_all[2]
        + beside_all[3]
        + beside_all[4]
        + beside_all[5]
    )
    lap = total - 6.0 * phi
    square = phi * phi
    summed = square[0] + square[1] + square[2] + square[3]
    under = 2.0 * ((zglob + offset).astype(jnp.float32) / depth - 0.5)
    rates = []
    for phase in range(4):
        psi = -(COMP[phase][0] * chem[0] + COMP[phase][1] * chem[1]) + LATENT[phase] * under
        rate = (
            KAPPA * lap[phase]
            - WELL * phi[phase] * (summed - square[phase])
            - 6.0 * phi[phase] * (1.0 - phi[phase]) * psi
        )
        rates.append(rate)
    mean_rate = (rates[0] + rates[1] + rates[2] + rates[3]) * 0.25
    return jnp.stack([phi[phase] + DT * (rates[phase] - mean_rate) for phase in range(4)])


def shape_fn(values):
    return values * values * (3.0 - 2.0 * values)


def chem_update(fields, side, phi_old, phi_new):
    chem = fields[4:]
    centre_d = DSOL + (DLIQ - DSOL) * fields[0]
    side_d = [DSOL + (DLIQ - DSOL) * s[0] for s in side]
    side_m = [s[4:] for s in side]
    flux = jnp.zeros_like(chem)
    for way in range(6):
        flux = flux + 0.5 * (centre_d + side_d[way]) * (side_m[way] - chem)
    delta = shape_fn(phi_new) - shape_fn(phi_old)
    result = []
    for comp in range(2):
        change = (
            COMP[0][comp] * delta[0]
            + COMP[1][comp] * delta[1]
            + COMP[2][comp] * delta[2]
            + COMP[3][comp] * delta[3]
        )
        result.append(chem[comp] + DT * flux[comp] - change)
    return jnp.stack(result)


def shards(labels, mu_start, front_blocks):
    cells_x, cells_y, cells_z = labels.shape
    lift = cells_z // 4
    bricks_y = lax.axis_size("gy")
    bricks_z = lax.axis_size("gz")
    depth = cells_z * bricks_z
    index_x = lax.axis_index("gx")
    index_y = lax.axis_index("gy")
    index_z = lax.axis_index("gz")
    bottom_brick = index_z == 0
    top_brick = index_z == bricks_z - 1
    base_z = index_z * cells_z
    rim_y = 4

    in_column = front_blocks[:, 0] == index_x

    def active(ypos, zpos):
        brick_y = (index_y + jnp.floor_divide(ypos, cells_y)) % bricks_y
        block = jnp.floor_divide(zpos, BZ)
        hits = (
            in_column[:, None, None]
            & (front_blocks[:, 1][:, None, None] == brick_y[None, :, None])
            & (front_blocks[:, 2][:, None, None] == block[None, None, :])
        )
        return jnp.any(hits, 0)

    low = lift - 4
    count = lift + 4
    stride = cells_z - low + count
    lane_z = jnp.arange(stride, dtype=jnp.int32)
    under_z = base_z + low + lane_z

    def step(ext, first_y, zpos, offset):
        size = ext.shape[2] - 2 * stride
        fields = ext[..., stride : stride + size]
        nrows = size // stride
        ypos = first_y + jnp.arange(nrows, dtype=jnp.int32)
        xlo, xhi = x_halos(fields)
        side = neighbours(ext, xlo, xhi, stride)
        on = active(ypos, zpos).reshape(-1)
        zflat = jnp.tile(under_z, nrows)
        phi_new = jnp.where(
            on[None, None],
            phase_update(fields, side, zflat, 0, depth),
            fields[:4],
        )
        mu_new = chem_update(fields, side, fields[:4], phi_new)
        return jnp.concatenate([phi_new, mu_new], 0)

    def lane_index(ext):
        return lax.broadcasted_iota(jnp.int32, ext.shape, 2) % stride

    def edge_at(ext, at, cond):
        up = jnp.concatenate([ext[..., :1], ext[..., :-1]], 2)
        return jnp.where(cond & (lane_index(ext) == at), up, ext)

    def edge_below(ext, at, cond):
        down = jnp.concatenate([ext[..., 1:], ext[..., -1:]], 2)
        return jnp.where(cond & (lane_index(ext) == at), down, ext)

    start = jnp.concatenate([labels.astype(jnp.float32)[None], mu_start], 0)
    nf = 4 + mu_start.shape[0]
    below_y = lax.ppermute(start[:, :, -rim_y:], "gy", ring("gy", 1))
    above_y = lax.ppermute(start[:, :, :rim_y], "gy", ring("gy", -1))
    wide = jnp.concatenate([below_y, start, above_y], 2)

    above = lax.ppermute(wide[..., :count].reshape(wide.shape[0], -1), "gz", line("gz", -1))
    ext = jnp.concatenate([wide[..., low:], above.reshape(wide.shape[:3] + (count,))], 3)
    ext = jnp.concatenate(
        [jnp.stack([(ext[0] == phase).astype(jnp.float32) for phase in range(4)]), ext[1:]], 0
    )
    rows = ext.shape[2]
    ext = ext.reshape(ext.shape[0], ext.shape[1], rows * stride)
    pre_z = base_z + low + lane_z
    post_z = pre_z - lift
    ext = edge_at(ext, cells_z - low, top_brick)
    ext = step(ext, 1 - rim_y, pre_z, 0)
    ext = edge_at(ext, cells_z - low, top_brick)
    ext = step(ext, 2 - rim_y, pre_z, 0)
    liquid = jnp.concatenate(
        [jnp.ones((1,) + ext.shape[1:], jnp.float32), jnp.zeros((nf - 1,) + ext.shape[1:], jnp.float32)], 0
    )
    ext = jnp.where(top_brick & (lane_index(ext) >= cells_z - low), liquid, ext)
    ext = edge_below(ext, lift - low - 1, bottom_brick)
    ext = edge_at(ext, cells_z + lift - low, top_brick)
    ext = step(ext, 3 - rim_y, post_z, lift)
    ext = edge_below(ext, lift - low - 1, bottom_brick)
    ext = edge_at(ext, cells_z + lift - low, top_brick)
    fields = step(ext, 4 - rim_y, post_z, lift)
    fields = fields.reshape(nf, cells_x, cells_y, stride)[..., lift - low : lift - low + cells_z]
    return (fields[:4], fields[4:])


def solution(mesh):
    placed = (P("gx", "gy", "gz"), P(None, "gx", "gy", "gz"), P())
    return jax.shard_map(
        shards,
        mesh=mesh,
        in_specs=placed,
        out_specs=(P(None, "gx", "gy", "gz"), P(None, "gx", "gy", "gz")),
        check_vma=False,
    )
```

```python
import jax
import jax.numpy as jnp
from jax import lax
from jax.sharding import PartitionSpec as P

BZ = 16


COMP = ((0.0, 0.0), (1.0, -0.5), (-0.5, 1.0), (-0.5, -0.5))
LATENT = (0.0, 1.0, 1.0, 1.0)
DT = 0.05
KAPPA = 1.5
WELL = 12.0
DLIQ = 3.0
DSOL = 0.3


def ring(axis, by):
    count = lax.axis_size(axis)
    return [(i, (i + by) % count) for i in range(count)]


def line(axis, by):
    count = lax.axis_size(axis)
    return [(i, i + by) for i in range(count) if 0 <= i + by < count]


def x_halos(block):
    if lax.axis_size("gx") == 2:
        pair = jnp.stack([block[:, -1], block[:, 0]])
        got = lax.ppermute(pair, "gx", ring("gx", 1))
        return got[0], got[1]
    xlo = lax.ppermute(block[:, -1], "gx", ring("gx", 1))
    xhi = lax.ppermute(block[:, 0], "gx", ring("gx", -1))
    return xlo, xhi


def neighbours(ext, xlo, xhi, stride):
    size = ext.shape[2] - 2 * stride
    fields = ext[..., stride : stride + size]
    return [
        jnp.concatenate([fields[:, 1:], xhi[:, None]], 1),
        jnp.concatenate([xlo[:, None], fields[:, :-1]], 1),
        ext[..., 2 * stride :],
        ext[..., :size],
        ext[..., stride + 1 : stride + 1 + size],
        ext[..., stride - 1 : stride - 1 + size],
    ]


def phase_update(fields, side, zglob, offset, depth):
    phi = fields[:4]
    chem = fields[4:]
    beside_all = [s[:4] for s in side]
    total = (
        beside_all[0]
        + beside_all[1]
        + beside_all[2]
        + beside_all[3]
        + beside_all[4]
        + beside_all[5]
    )
    lap = total - 6.0 * phi
    square = phi * phi
    summed = square[0] + square[1] + square[2] + square[3]
    under = 2.0 * ((zglob + offset).astype(jnp.float32) / depth - 0.5)
    rates = []
    for phase in range(4):
        psi = -(COMP[phase][0] * chem[0] + COMP[phase][1] * chem[1]) + LATENT[phase] * under
        rate = (
            KAPPA * lap[phase]
            - WELL * phi[phase] * (summed - square[phase])
            - 6.0 * phi[phase] * (1.0 - phi[phase]) * psi
        )
        rates.append(rate)
    mean_rate = (rates[0] + rates[1] + rates[2] + rates[3]) * 0.25
    return jnp.stack([phi[phase] + DT * (rates[phase] - mean_rate) for phase in range(4)])


def shape_fn(values):
    return values * values * (3.0 - 2.0 * values)


def chem_update(fields, side, phi_old, phi_new):
    chem = fields[4:]
    centre_d = DSOL + (DLIQ - DSOL) * fields[0]
    side_d = [DSOL + (DLIQ - DSOL) * s[0] for s in side]
    side_m = [s[4:] for s in side]
    flux = jnp.zeros_like(chem)
    for way in range(6):
        flux = flux + 0.5 * (centre_d + side_d[way]) * (side_m[way] - chem)
    delta = shape_fn(phi_new) - shape_fn(phi_old)
    result = []
    for comp in range(2):
        change = (
            COMP[0][comp] * delta[0]
            + COMP[1][comp] * delta[1]
            + COMP[2][comp] * delta[2]
            + COMP[3][comp] * delta[3]
        )
        result.append(chem[comp] + DT * flux[comp] - change)
    return jnp.stack(result)


def shards(labels, mu_start, front_blocks):
    cells_x, cells_y, cells_z = labels.shape
    lift = cells_z // 4
    bricks_y = lax.axis_size("gy")
    bricks_z = lax.axis_size("gz")
    depth = cells_z * bricks_z
    index_x = lax.axis_index("gx")
    index_y = lax.axis_index("gy")
    index_z = lax.axis_index("gz")
    bottom_brick = index_z == 0
    top_brick = index_z == bricks_z - 1
    base_z = index_z * cells_z
    rim_y = 4

    in_column = front_blocks[:, 0] == index_x

    def active(ypos, zpos):
        brick_y = (index_y + jnp.floor_divide(ypos, cells_y)) % bricks_y
        block = jnp.floor_divide(zpos, BZ)
        hits = (
            in_column[:, None, None]
            & (front_blocks[:, 1][:, None, None] == brick_y[None, :, None])
            & (front_blocks[:, 2][:, None, None] == block[None, None, :])
        )
        return jnp.any(hits, 0)

    low = lift - 4
    count = lift + 4
    stride = cells_z - low + count
    lane_z = jnp.arange(stride, dtype=jnp.int32)
    under_z = base_z + low + lane_z

    def step(ext, first_y, zpos, offset):
        size = ext.shape[2] - 2 * stride
        fields = ext[..., stride : stride + size]
        nrows = size // stride
        ypos = first_y + jnp.arange(nrows, dtype=jnp.int32)
        xlo, xhi = x_halos(fields)
        near = [
            ext[..., 2 * stride :],
            ext[..., :size],
            ext[..., stride + 1 : stride + 1 + size],
            ext[..., stride - 1 : stride - 1 + size],
        ]
        phi = fields[:4]
        chem = fields[4:]
        centre_d = DSOL + (DLIQ - DSOL) * fields[0]
        part_lap = near[0][:4] + near[1][:4] + near[2][:4] + near[3][:4]
        part_flux = jnp.zeros_like(chem)
        for s in near:
            part_flux = part_flux + 0.5 * (centre_d + (DSOL + (DLIQ - DSOL) * s[0])) * (s[4:] - chem)
        part_lap, part_flux = lax.optimization_barrier((part_lap, part_flux))
        xp = jnp.concatenate([fields[:, 1:], xhi[:, None]], 1)
        xm = jnp.concatenate([xlo[:, None], fields[:, :-1]], 1)
        total = part_lap + xp[:4] + xm[:4]
        lap = total - 6.0 * phi
        square = phi * phi
        summed = square[0] + square[1] + square[2] + square[3]
        under = 2.0 * (jnp.tile(under_z, nrows).astype(jnp.float32) / depth - 0.5)
        rates = []
        for phase in range(4):
            psi = -(COMP[phase][0] * chem[0] + COMP[phase][1] * chem[1]) + LATENT[phase] * under
            rate = (
                KAPPA * lap[phase]
                - WELL * phi[phase] * (summed - square[phase])
                - 6.0 * phi[phase] * (1.0 - phi[phase]) * psi
            )
            rates.append(rate)
        mean_rate = (rates[0] + rates[1] + rates[2] + rates[3]) * 0.25
        stepped = jnp.stack([phi[phase] + DT * (rates[phase] - mean_rate) for phase in range(4)])
        on = active(ypos, zpos).reshape(-1)
        phi_new = jnp.where(on[None, None], stepped, phi)
        flux = part_flux
        for s in (xp, xm):
            flux = flux + 0.5 * (centre_d + (DSOL + (DLIQ - DSOL) * s[0])) * (s[4:] - chem)
        delta = shape_fn(phi_new) - shape_fn(phi)
        result = []
        for comp in range(2):
            change = (
                COMP[0][comp] * delta[0]
                + COMP[1][comp] * delta[1]
                + COMP[2][comp] * delta[2]
                + COMP[3][comp] * delta[3]
            )
            result.append(chem[comp] + DT * flux[comp] - change)
        return jnp.concatenate([phi_new, jnp.stack(result)], 0)

    def lane_index(ext):
        return lax.broadcasted_iota(jnp.int32, ext.shape, 2) % stride

    def edge_at(ext, at, cond):
        up = jnp.concatenate([ext[..., :1], ext[..., :-1]], 2)
        return jnp.where(cond & (lane_index(ext) == at), up, ext)

    def edge_below(ext, at, cond):
        down = jnp.concatenate([ext[..., 1:], ext[..., -1:]], 2)
        return jnp.where(cond & (lane_index(ext) == at), down, ext)

    start = jnp.concatenate([labels.astype(jnp.float32)[None], mu_start], 0)
    nf = 4 + mu_start.shape[0]
    below_y = lax.ppermute(start[:, :, -rim_y:], "gy", ring("gy", 1))
    above_y = lax.ppermute(start[:, :, :rim_y], "gy", ring("gy", -1))
    wide = jnp.concatenate([below_y, start, above_y], 2)

    above = lax.ppermute(wide[..., :count].reshape(wide.shape[0], -1), "gz", line("gz", -1))
    ext = jnp.concatenate([wide[..., low:], above.reshape(wide.shape[:3] + (count,))], 3)
    ext = jnp.concatenate(
        [jnp.stack([(ext[0] == phase).astype(jnp.float32) for phase in range(4)]), ext[1:]], 0
    )
    rows = ext.shape[2]
    ext = ext.reshape(ext.shape[0], ext.shape[1], rows * stride)
    pre_z = base_z + low + lane_z
    post_z = pre_z - lift
    ext = edge_at(ext, cells_z - low, top_brick)
    ext = step(ext, 1 - rim_y, pre_z, 0)
    ext = edge_at(ext, cells_z - low, top_brick)
    ext = step(ext, 2 - rim_y, pre_z, 0)
    liquid = jnp.concatenate(
        [jnp.ones((1,) + ext.shape[1:], jnp.float32), jnp.zeros((nf - 1,) + ext.shape[1:], jnp.float32)], 0
    )
    ext = jnp.where(top_brick & (lane_index(ext) >= cells_z - low), liquid, ext)
    ext = edge_below(ext, lift - low - 1, bottom_brick)
    ext = edge_at(ext, cells_z + lift - low, top_brick)
    ext = step(ext, 3 - rim_y, post_z, lift)
    ext = edge_below(ext, lift - low - 1, bottom_brick)
    ext = edge_at(ext, cells_z + lift - low, top_brick)
    fields = step(ext, 4 - rim_y, post_z, lift)
    fields = fields.reshape(nf, cells_x, cells_y, stride)[..., lift - low : lift - low + cells_z]
    return (fields[:4], fields[4:])


def solution(mesh):
    placed = (P("gx", "gy", "gz"), P(None, "gx", "gy", "gz"), P())
    return jax.shard_map(
        shards,
        mesh=mesh,
        in_specs=placed,
        out_specs=(P(None, "gx", "gy", "gz"), P(None, "gx", "gy", "gz")),
        check_vma=False,
    )
```

```python
import jax
import jax.numpy as jnp
from jax import lax
from jax.sharding import PartitionSpec as P

BZ = 16


COMP = ((0.0, 0.0), (1.0, -0.5), (-0.5, 1.0), (-0.5, -0.5))
LATENT = (0.0, 1.0, 1.0, 1.0)
DT = 0.05
KAPPA = 1.5
WELL = 12.0
DLIQ = 3.0
DSOL = 0.3


def ring(axis, by):
    count = lax.axis_size(axis)
    return [(i, (i + by) % count) for i in range(count)]


def line(axis, by):
    count = lax.axis_size(axis)
    return [(i, i + by) for i in range(count) if 0 <= i + by < count]


def x_halos(block):
    if lax.axis_size("gx") == 2:
        pair = jnp.stack([block[:, -1], block[:, 0]])
        got = lax.ppermute(pair, "gx", ring("gx", 1))
        return got[0], got[1]
    xlo = lax.ppermute(block[:, -1], "gx", ring("gx", 1))
    xhi = lax.ppermute(block[:, 0], "gx", ring("gx", -1))
    return xlo, xhi


def neighbours(ext, xlo, xhi, stride):
    size = ext.shape[2] - 2 * stride
    fields = ext[..., stride : stride + size]
    return [
        jnp.concatenate([fields[:, 1:], xhi[:, None]], 1),
        jnp.concatenate([xlo[:, None], fields[:, :-1]], 1),
        ext[..., 2 * stride :],
        ext[..., :size],
        ext[..., stride + 1 : stride + 1 + size],
        ext[..., stride - 1 : stride - 1 + size],
    ]


def phase_update(fields, side, zglob, offset, depth):
    phi = fields[:4]
    chem = fields[4:]
    beside_all = [s[:4] for s in side]
    total = (
        beside_all[0]
        + beside_all[1]
        + beside_all[2]
        + beside_all[3]
        + beside_all[4]
        + beside_all[5]
    )
    lap = total - 6.0 * phi
    square = phi * phi
    summed = square[0] + square[1] + square[2] + square[3]
    under = 2.0 * ((zglob + offset).astype(jnp.float32) / depth - 0.5)
    rates = []
    for phase in range(4):
        psi = -(COMP[phase][0] * chem[0] + COMP[phase][1] * chem[1]) + LATENT[phase] * under
        rate = (
            KAPPA * lap[phase]
            - WELL * phi[phase] * (summed - square[phase])
            - 6.0 * phi[phase] * (1.0 - phi[phase]) * psi
        )
        rates.append(rate)
    mean_rate = (rates[0] + rates[1] + rates[2] + rates[3]) * 0.25
    return jnp.stack([phi[phase] + DT * (rates[phase] - mean_rate) for phase in range(4)])


def shape_fn(values):
    return values * values * (3.0 - 2.0 * values)


def chem_update(fields, side, phi_old, phi_new):
    chem = fields[4:]
    centre_d = DSOL + (DLIQ - DSOL) * fields[0]
    side_d = [DSOL + (DLIQ - DSOL) * s[0] for s in side]
    side_m = [s[4:] for s in side]
    flux = jnp.zeros_like(chem)
    for way in range(6):
        flux = flux + 0.5 * (centre_d + side_d[way]) * (side_m[way] - chem)
    delta = shape_fn(phi_new) - shape_fn(phi_old)
    result = []
    for comp in range(2):
        change = (
            COMP[0][comp] * delta[0]
            + COMP[1][comp] * delta[1]
            + COMP[2][comp] * delta[2]
            + COMP[3][comp] * delta[3]
        )
        result.append(chem[comp] + DT * flux[comp] - change)
    return jnp.stack(result)


def shards(labels, mu_start, front_blocks):
    cells_x, cells_y, cells_z = labels.shape
    lift = cells_z // 4
    bricks_y = lax.axis_size("gy")
    bricks_z = lax.axis_size("gz")
    depth = cells_z * bricks_z
    index_x = lax.axis_index("gx")
    index_y = lax.axis_index("gy")
    index_z = lax.axis_index("gz")
    bottom_brick = index_z == 0
    top_brick = index_z == bricks_z - 1
    base_z = index_z * cells_z
    rim_y = 4

    in_column = front_blocks[:, 0] == index_x

    def active(ypos, zpos):
        brick_y = (index_y + jnp.floor_divide(ypos, cells_y)) % bricks_y
        block = jnp.floor_divide(zpos, BZ)
        hits = (
            in_column[:, None, None]
            & (front_blocks[:, 1][:, None, None] == brick_y[None, :, None])
            & (front_blocks[:, 2][:, None, None] == block[None, None, :])
        )
        return jnp.any(hits, 0)

    low = lift - 4
    count = lift + 4
    stride = cells_z - low + count
    lane_z = jnp.arange(stride, dtype=jnp.int32)
    under_z = base_z + low + lane_z

    def step(ext, first_y, zpos, offset):
        size = ext.shape[2] - 2 * stride
        fields = ext[..., stride : stride + size]
        nrows = size // stride
        ypos = first_y + jnp.arange(nrows, dtype=jnp.int32)
        xlo, xhi = x_halos(fields)
        side = neighbours(ext, xlo, xhi, stride)
        on = active(ypos, zpos).reshape(-1)
        zflat = jnp.tile(under_z, nrows)
        phi_new = jnp.where(
            on[None, None],
            phase_update(fields, side, zflat, 0, depth),
            fields[:4],
        )
        mu_new = chem_update(fields, side, fields[:4], phi_new)
        return jnp.concatenate([phi_new, mu_new], 0)

    def lane_index(ext):
        return lax.broadcasted_iota(jnp.int32, ext.shape, 2) % stride

    def edge_at(ext, at, cond):
        up = jnp.concatenate([ext[..., :1], ext[..., :-1]], 2)
        return jnp.where(cond & (lane_index(ext) == at), up, ext)

    def edge_below(ext, at, cond):
        down = jnp.concatenate([ext[..., 1:], ext[..., -1:]], 2)
        return jnp.where(cond & (lane_index(ext) == at), down, ext)

    start = jnp.concatenate([labels.astype(jnp.float32)[None], mu_start], 0)
    nf = 4 + mu_start.shape[0]
    below_y = lax.ppermute(start[:, :, -rim_y:], "gy", ring("gy", 1))
    above_y = lax.ppermute(start[:, :, :rim_y], "gy", ring("gy", -1))
    wide = jnp.concatenate([below_y, start, above_y], 2)

    above = lax.ppermute(wide[..., :count].reshape(wide.shape[0], -1), "gz", line("gz", -1))
    ext = jnp.concatenate([wide[..., low:], above.reshape(wide.shape[:3] + (count,))], 3)
    ext = jnp.concatenate(
        [jnp.stack([(ext[0] == phase).astype(jnp.float32) for phase in range(4)]), ext[1:]], 0
    )
    rows = ext.shape[2]
    ext = ext.reshape(ext.shape[0], ext.shape[1], rows * stride)
    pre_z = base_z + low + lane_z
    post_z = pre_z - lift
    ext = edge_at(ext, cells_z - low, top_brick)
    ext = step(ext, 1 - rim_y, pre_z, 0)
    ext = edge_at(ext, cells_z - low, top_brick)
    ext = step(ext, 2 - rim_y, pre_z, 0)
    liquid = jnp.where(lax.broadcasted_iota(jnp.int32, ext.shape, 0) == 0, 1.0, 0.0).astype(jnp.float32)
    ext = jnp.where(top_brick & (lane_index(ext) >= cells_z - low), liquid, ext)
    ext = edge_below(ext, lift - low - 1, bottom_brick)
    ext = edge_at(ext, cells_z + lift - low, top_brick)
    ext = step(ext, 3 - rim_y, post_z, lift)
    ext = edge_below(ext, lift - low - 1, bottom_brick)
    ext = edge_at(ext, cells_z + lift - low, top_brick)
    fields = step(ext, 4 - rim_y, post_z, lift)
    fields = fields.reshape(nf, cells_x, cells_y, stride)[..., lift - low : lift - low + cells_z]
    return (fields[:4], fields[4:])


def solution(mesh):
    placed = (P("gx", "gy", "gz"), P(None, "gx", "gy", "gz"), P())
    return jax.shard_map(
        shards,
        mesh=mesh,
        in_specs=placed,
        out_specs=(P(None, "gx", "gy", "gz"), P(None, "gx", "gy", "gz")),
        check_vma=False,
    )
```

```python
import jax
import jax.numpy as jnp
from jax import lax
from jax.sharding import PartitionSpec as P

BZ = 16


COMP = ((0.0, 0.0), (1.0, -0.5), (-0.5, 1.0), (-0.5, -0.5))
LATENT = (0.0, 1.0, 1.0, 1.0)
DT = 0.05
KAPPA = 1.5
WELL = 12.0
DLIQ = 3.0
DSOL = 0.3


def ring(axis, by):
    count = lax.axis_size(axis)
    return [(i, (i + by) % count) for i in range(count)]


def line(axis, by):
    count = lax.axis_size(axis)
    return [(i, i + by) for i in range(count) if 0 <= i + by < count]


def x_halos(block):
    if lax.axis_size("gx") == 2:
        pair = jnp.stack([block[:, -1], block[:, 0]])
        got = lax.ppermute(pair, "gx", ring("gx", 1))
        return got[0], got[1]
    xlo = lax.ppermute(block[:, -1], "gx", ring("gx", 1))
    xhi = lax.ppermute(block[:, 0], "gx", ring("gx", -1))
    return xlo, xhi


def neighbours(ext, xlo, xhi, stride):
    size = ext.shape[2] - 2 * stride
    fields = ext[..., stride : stride + size]
    return [
        jnp.concatenate([fields[:, 1:], xhi[:, None]], 1),
        jnp.concatenate([xlo[:, None], fields[:, :-1]], 1),
        ext[..., 2 * stride :],
        ext[..., :size],
        ext[..., stride + 1 : stride + 1 + size],
        ext[..., stride - 1 : stride - 1 + size],
    ]


def phase_update(fields, side, zglob, offset, depth):
    phi = fields[:4]
    chem = fields[4:]
    beside_all = [s[:4] for s in side]
    total = (
        beside_all[0]
        + beside_all[1]
        + beside_all[2]
        + beside_all[3]
        + beside_all[4]
        + beside_all[5]
    )
    lap = total - 6.0 * phi
    square = phi * phi
    summed = square[0] + square[1] + square[2] + square[3]
    under = 2.0 * ((zglob + offset).astype(jnp.float32) / depth - 0.5)
    rates = []
    for phase in range(4):
        psi = -(COMP[phase][0] * chem[0] + COMP[phase][1] * chem[1]) + LATENT[phase] * under
        rate = (
            KAPPA * lap[phase]
            - WELL * phi[phase] * (summed - square[phase])
            - 6.0 * phi[phase] * (1.0 - phi[phase]) * psi
        )
        rates.append(rate)
    mean_rate = (rates[0] + rates[1] + rates[2] + rates[3]) * 0.25
    return jnp.stack([phi[phase] + DT * (rates[phase] - mean_rate) for phase in range(4)])


def shape_fn(values):
    return values * values * (3.0 - 2.0 * values)


def chem_update(fields, side, phi_old, phi_new):
    chem = fields[4:]
    centre_d = DSOL + (DLIQ - DSOL) * fields[0]
    side_d = [DSOL + (DLIQ - DSOL) * s[0] for s in side]
    side_m = [s[4:] for s in side]
    flux = jnp.zeros_like(chem)
    for way in range(6):
        flux = flux + 0.5 * (centre_d + side_d[way]) * (side_m[way] - chem)
    delta = shape_fn(phi_new) - shape_fn(phi_old)
    result = []
    for comp in range(2):
        change = (
            COMP[0][comp] * delta[0]
            + COMP[1][comp] * delta[1]
            + COMP[2][comp] * delta[2]
            + COMP[3][comp] * delta[3]
        )
        result.append(chem[comp] + DT * flux[comp] - change)
    return jnp.stack(result)


def shards(labels, mu_start, front_blocks):
    cells_x, cells_y, cells_z = labels.shape
    lift = cells_z // 4
    bricks_y = lax.axis_size("gy")
    bricks_z = lax.axis_size("gz")
    depth = cells_z * bricks_z
    index_x = lax.axis_index("gx")
    index_y = lax.axis_index("gy")
    index_z = lax.axis_index("gz")
    bottom_brick = index_z == 0
    top_brick = index_z == bricks_z - 1
    base_z = index_z * cells_z
    rim_y = 4

    in_column = front_blocks[:, 0] == index_x

    def active(ypos, zpos):
        brick_y = (index_y + jnp.floor_divide(ypos, cells_y)) % bricks_y
        block = jnp.floor_divide(zpos, BZ)
        hits = (
            in_column[:, None, None]
            & (front_blocks[:, 1][:, None, None] == brick_y[None, :, None])
            & (front_blocks[:, 2][:, None, None] == block[None, None, :])
        )
        return jnp.any(hits, 0)

    low = lift - 4
    count = lift + 4
    stride = cells_z - low + count
    lane_z = jnp.arange(stride, dtype=jnp.int32)
    under_z = base_z + low + lane_z

    def step(ext, first_y, zpos, offset):
        size = ext.shape[2] - 2 * stride
        fields = ext[..., stride : stride + size]
        nrows = size // stride
        ypos = first_y + jnp.arange(nrows, dtype=jnp.int32)
        xlo, xhi = x_halos(fields)
        side = neighbours(ext, xlo, xhi, stride)
        on = active(ypos, zpos).reshape(-1)
        zflat = jnp.tile(under_z, nrows)
        phi_new = jnp.where(
            on[None, None],
            phase_update(fields, side, zflat, 0, depth),
            fields[:4],
        )
        mu_new = chem_update(fields, side, fields[:4], phi_new)
        return jnp.concatenate([phi_new, mu_new], 0)

    def lane_index(ext):
        return lax.broadcasted_iota(jnp.int32, ext.shape, 2) % stride

    def edge_at(ext, at, cond):
        up = jnp.concatenate([ext[..., :1], ext[..., :-1]], 2)
        return jnp.where(cond & (lane_index(ext) == at), up, ext)

    def edge_below(ext, at, cond):
        down = jnp.concatenate([ext[..., 1:], ext[..., -1:]], 2)
        return jnp.where(cond & (lane_index(ext) == at), down, ext)

    start = jnp.concatenate([labels.astype(jnp.float32)[None], mu_start], 0)
    nf = 4 + mu_start.shape[0]
    below_y = lax.ppermute(start[:, :, -rim_y:], "gy", ring("gy", 1))
    above_y = lax.ppermute(start[:, :, :rim_y], "gy", ring("gy", -1))
    wide = jnp.concatenate([below_y, start, above_y], 2)

    above = lax.ppermute(wide[..., :count].reshape(wide.shape[0], -1), "gz", line("gz", -1))
    ext = jnp.concatenate([wide[..., low:], above.reshape(wide.shape[:3] + (count,))], 3)
    ext = jnp.concatenate(
        [jnp.stack([(ext[0] == phase).astype(jnp.float32) for phase in range(4)]), ext[1:]], 0
    )
    rows = ext.shape[2]
    ext = ext.reshape(ext.shape[0], ext.shape[1], rows * stride)
    pre_z = base_z + low + lane_z
    post_z = pre_z - lift
    ext = edge_at(ext, cells_z - low, top_brick)
    ext = step(ext, 1 - rim_y, pre_z, 0)
    ext = edge_at(ext, cells_z - low, top_brick)
    ext = step(ext, 2 - rim_y, pre_z, 0)
    liquid = jnp.where(lax.broadcasted_iota(jnp.int32, ext.shape, 0) == 0, 1.0, 0.0).astype(jnp.float32)
    ext = jnp.where(top_brick & (lane_index(ext) >= cells_z - low), liquid, ext)
    ext = edge_below(ext, lift - low - 1, bottom_brick)
    ext = edge_at(ext, cells_z + lift - low, top_brick)
    ext = step(ext, 3 - rim_y, post_z, lift)
    ext = edge_below(ext, lift - low - 1, bottom_brick)
    ext = edge_at(ext, cells_z + lift - low, top_brick)
    grid = ext.reshape(nf, cells_x, cells_y + 2, stride)
    first = lift - low
    fields = grid[:, :, 1:-1, first : first + cells_z]
    xlo, xhi = x_halos(fields)
    side = [
        jnp.concatenate([fields[:, 1:], xhi[:, None]], 1),
        jnp.concatenate([xlo[:, None], fields[:, :-1]], 1),
        grid[:, :, 2:, first : first + cells_z],
        grid[:, :, :-2, first : first + cells_z],
        grid[:, :, 1:-1, first + 1 : first + 1 + cells_z],
        grid[:, :, 1:-1, first - 1 : first - 1 + cells_z],
    ]
    ypos = jnp.arange(cells_y, dtype=jnp.int32)
    zlast = post_z[first : first + cells_z]
    phi_new = jnp.where(
        active(ypos, zlast)[None, None],
        phase_update(fields, side, under_z[first : first + cells_z], 0, depth),
        fields[:4],
    )
    mu_new = chem_update(fields, side, fields[:4], phi_new)
    return (phi_new, mu_new)


def solution(mesh):
    placed = (P("gx", "gy", "gz"), P(None, "gx", "gy", "gz"), P())
    return jax.shard_map(
        shards,
        mesh=mesh,
        in_specs=placed,
        out_specs=(P(None, "gx", "gy", "gz"), P(None, "gx", "gy", "gz")),
        check_vma=False,
    )
```

```python
import jax
import jax.numpy as jnp
from jax import lax
from jax.sharding import PartitionSpec as P

BZ = 16


COMP = ((0.0, 0.0), (1.0, -0.5), (-0.5, 1.0), (-0.5, -0.5))
LATENT = (0.0, 1.0, 1.0, 1.0)
DT = 0.05
KAPPA = 1.5
WELL = 12.0
DLIQ = 3.0
DSOL = 0.3


def ring(axis, by):
    count = lax.axis_size(axis)
    return [(i, (i + by) % count) for i in range(count)]


def line(axis, by):
    count = lax.axis_size(axis)
    return [(i, i + by) for i in range(count) if 0 <= i + by < count]


def x_halos(block):
    if lax.axis_size("gx") == 2:
        pair = jnp.stack([block[:, -1], block[:, 0]])
        got = lax.ppermute(pair, "gx", ring("gx", 1))
        return got[0], got[1]
    xlo = lax.ppermute(block[:, -1], "gx", ring("gx", 1))
    xhi = lax.ppermute(block[:, 0], "gx", ring("gx", -1))
    return xlo, xhi


def neighbours(ext, xlo, xhi, stride):
    size = ext.shape[2] - 2 * stride
    fields = ext[..., stride : stride + size]
    return [
        jnp.concatenate([fields[:, 1:], xhi[:, None]], 1),
        jnp.concatenate([xlo[:, None], fields[:, :-1]], 1),
        ext[..., 2 * stride :],
        ext[..., :size],
        ext[..., stride + 1 : stride + 1 + size],
        ext[..., stride - 1 : stride - 1 + size],
    ]


def phase_update(fields, side, zglob, offset, depth):
    phi = fields[:4]
    chem = fields[4:]
    beside_all = [s[:4] for s in side]
    total = (
        beside_all[0]
        + beside_all[1]
        + beside_all[2]
        + beside_all[3]
        + beside_all[4]
        + beside_all[5]
    )
    lap = total - 6.0 * phi
    square = phi * phi
    summed = square[0] + square[1] + square[2] + square[3]
    under = 2.0 * ((zglob + offset).astype(jnp.float32) / depth - 0.5)
    rates = []
    for phase in range(4):
        psi = -(COMP[phase][0] * chem[0] + COMP[phase][1] * chem[1]) + LATENT[phase] * under
        rate = (
            KAPPA * lap[phase]
            - WELL * phi[phase] * (summed - square[phase])
            - 6.0 * phi[phase] * (1.0 - phi[phase]) * psi
        )
        rates.append(rate)
    mean_rate = (rates[0] + rates[1] + rates[2] + rates[3]) * 0.25
    return jnp.stack([phi[phase] + DT * (rates[phase] - mean_rate) for phase in range(4)])


def shape_fn(values):
    return values * values * (3.0 - 2.0 * values)


def chem_update(fields, side, phi_old, phi_new):
    chem = fields[4:]
    centre_d = DSOL + (DLIQ - DSOL) * fields[0]
    side_d = [DSOL + (DLIQ - DSOL) * s[0] for s in side]
    side_m = [s[4:] for s in side]
    flux = jnp.zeros_like(chem)
    for way in range(6):
        flux = flux + 0.5 * (centre_d + side_d[way]) * (side_m[way] - chem)
    delta = shape_fn(phi_new) - shape_fn(phi_old)
    result = []
    for comp in range(2):
        change = (
            COMP[0][comp] * delta[0]
            + COMP[1][comp] * delta[1]
            + COMP[2][comp] * delta[2]
            + COMP[3][comp] * delta[3]
        )
        result.append(chem[comp] + DT * flux[comp] - change)
    return jnp.stack(result)


def shards(labels, mu_start, front_blocks):
    cells_x, cells_y, cells_z = labels.shape
    lift = cells_z // 4
    bricks_y = lax.axis_size("gy")
    bricks_z = lax.axis_size("gz")
    depth = cells_z * bricks_z
    index_x = lax.axis_index("gx")
    index_y = lax.axis_index("gy")
    index_z = lax.axis_index("gz")
    bottom_brick = index_z == 0
    top_brick = index_z == bricks_z - 1
    base_z = index_z * cells_z
    rim_y = 4

    in_column = front_blocks[:, 0] == index_x

    def active(ypos, zpos):
        brick_y = (index_y + jnp.floor_divide(ypos, cells_y)) % bricks_y
        block = jnp.floor_divide(zpos, BZ)
        hits = (
            in_column[:, None, None]
            & (front_blocks[:, 1][:, None, None] == brick_y[None, :, None])
            & (front_blocks[:, 2][:, None, None] == block[None, None, :])
        )
        return jnp.any(hits, 0)

    low = lift - 4
    count = lift + 4
    stride = cells_z - low + count
    lane_z = jnp.arange(stride, dtype=jnp.int32)
    under_z = base_z + low + lane_z

    def step(ext, first_y, zpos, offset, x_rim=False):
        size = ext.shape[2] - 2 * stride
        if x_rim:
            rim = ext[..., stride : stride + size]
            xlo, xhi = rim[:, 0], rim[:, -1]
            ext = ext[:, 1:-1]
        fields = ext[..., stride : stride + size]
        nrows = size // stride
        ypos = first_y + jnp.arange(nrows, dtype=jnp.int32)
        if not x_rim:
            xlo, xhi = x_halos(fields)
        side = neighbours(ext, xlo, xhi, stride)
        on = active(ypos, zpos).reshape(-1)
        zflat = jnp.tile(under_z, nrows)
        phi_new = jnp.where(
            on[None, None],
            phase_update(fields, side, zflat, 0, depth),
            fields[:4],
        )
        mu_new = chem_update(fields, side, fields[:4], phi_new)
        return jnp.concatenate([phi_new, mu_new], 0)

    def lane_index(ext):
        return lax.broadcasted_iota(jnp.int32, ext.shape, 2) % stride

    def edge_at(ext, at, cond):
        up = jnp.concatenate([ext[..., :1], ext[..., :-1]], 2)
        return jnp.where(cond & (lane_index(ext) == at), up, ext)

    def edge_below(ext, at, cond):
        down = jnp.concatenate([ext[..., 1:], ext[..., -1:]], 2)
        return jnp.where(cond & (lane_index(ext) == at), down, ext)

    start = jnp.concatenate([labels.astype(jnp.float32)[None], mu_start], 0)
    nf = 4 + mu_start.shape[0]
    xlo, xhi = x_halos(start)
    start = jnp.concatenate([xlo[:, None], start, xhi[:, None]], 1)
    below_y = lax.ppermute(start[:, :, -rim_y:], "gy", ring("gy", 1))
    above_y = lax.ppermute(start[:, :, :rim_y], "gy", ring("gy", -1))
    wide = jnp.concatenate([below_y, start, above_y], 2)

    above = lax.ppermute(wide[..., :count].reshape(wide.shape[0], -1), "gz", line("gz", -1))
    ext = jnp.concatenate([wide[..., low:], above.reshape(wide.shape[:3] + (count,))], 3)
    ext = jnp.concatenate(
        [jnp.stack([(ext[0] == phase).astype(jnp.float32) for phase in range(4)]), ext[1:]], 0
    )
    rows = ext.shape[2]
    ext = ext.reshape(ext.shape[0], ext.shape[1], rows * stride)
    pre_z = base_z + low + lane_z
    post_z = pre_z - lift
    ext = edge_at(ext, cells_z - low, top_brick)
    ext = step(ext, 1 - rim_y, pre_z, 0, x_rim=True)
    ext = edge_at(ext, cells_z - low, top_brick)
    ext = step(ext, 2 - rim_y, pre_z, 0)
    liquid = jnp.where(lax.broadcasted_iota(jnp.int32, ext.shape, 0) == 0, 1.0, 0.0).astype(jnp.float32)
    ext = jnp.where(top_brick & (lane_index(ext) >= cells_z - low), liquid, ext)
    ext = edge_below(ext, lift - low - 1, bottom_brick)
    ext = edge_at(ext, cells_z + lift - low, top_brick)
    ext = step(ext, 3 - rim_y, post_z, lift)
    ext = edge_below(ext, lift - low - 1, bottom_brick)
    ext = edge_at(ext, cells_z + lift - low, top_brick)
    grid = ext.reshape(nf, cells_x, cells_y + 2, stride)
    first = lift - low
    fields = grid[:, :, 1:-1, first : first + cells_z]
    xlo, xhi = x_halos(fields)
    side = [
        jnp.concatenate([fields[:, 1:], xhi[:, None]], 1),
        jnp.concatenate([xlo[:, None], fields[:, :-1]], 1),
        grid[:, :, 2:, first : first + cells_z],
        grid[:, :, :-2, first : first + cells_z],
        grid[:, :, 1:-1, first + 1 : first + 1 + cells_z],
        grid[:, :, 1:-1, first - 1 : first - 1 + cells_z],
    ]
    ypos = jnp.arange(cells_y, dtype=jnp.int32)
    zlast = post_z[first : first + cells_z]
    phi_new = jnp.where(
        active(ypos, zlast)[None, None],
        phase_update(fields, side, under_z[first : first + cells_z], 0, depth),
        fields[:4],
    )
    mu_new = chem_update(fields, side, fields[:4], phi_new)
    return (phi_new, mu_new)


def solution(mesh):
    placed = (P("gx", "gy", "gz"), P(None, "gx", "gy", "gz"), P())
    return jax.shard_map(
        shards,
        mesh=mesh,
        in_specs=placed,
        out_specs=(P(None, "gx", "gy", "gz"), P(None, "gx", "gy", "gz")),
        check_vma=False,
    )
```

```python
import jax
import jax.numpy as jnp
from jax import lax
from jax.sharding import PartitionSpec as P

BZ = 16


COMP = ((0.0, 0.0), (1.0, -0.5), (-0.5, 1.0), (-0.5, -0.5))
LATENT = (0.0, 1.0, 1.0, 1.0)
DT = 0.05
KAPPA = 1.5
WELL = 12.0
DLIQ = 3.0
DSOL = 0.3


def ring(axis, by):
    count = lax.axis_size(axis)
    return [(i, (i + by) % count) for i in range(count)]


def line(axis, by):
    count = lax.axis_size(axis)
    return [(i, i + by) for i in range(count) if 0 <= i + by < count]


def x_halos(block):
    if lax.axis_size("gx") == 2:
        pair = jnp.stack([block[:, -1], block[:, 0]])
        got = lax.ppermute(pair, "gx", ring("gx", 1))
        return got[0], got[1]
    xlo = lax.ppermute(block[:, -1], "gx", ring("gx", 1))
    xhi = lax.ppermute(block[:, 0], "gx", ring("gx", -1))
    return xlo, xhi


def neighbours(ext, xlo, xhi, stride):
    size = ext.shape[2] - 2 * stride
    fields = ext[..., stride : stride + size]
    return [
        jnp.concatenate([fields[:, 1:], xhi[:, None]], 1),
        jnp.concatenate([xlo[:, None], fields[:, :-1]], 1),
        ext[..., 2 * stride :],
        ext[..., :size],
        ext[..., stride + 1 : stride + 1 + size],
        ext[..., stride - 1 : stride - 1 + size],
    ]


def phase_update(fields, side, zglob, offset, depth):
    phi = fields[:4]
    chem = fields[4:]
    beside_all = [s[:4] for s in side]
    total = (
        beside_all[0]
        + beside_all[1]
        + beside_all[2]
        + beside_all[3]
        + beside_all[4]
        + beside_all[5]
    )
    lap = total - 6.0 * phi
    square = phi * phi
    summed = square[0] + square[1] + square[2] + square[3]
    under = 2.0 * ((zglob + offset).astype(jnp.float32) / depth - 0.5)
    rates = []
    for phase in range(4):
        psi = -(COMP[phase][0] * chem[0] + COMP[phase][1] * chem[1]) + LATENT[phase] * under
        rate = (
            KAPPA * lap[phase]
            - WELL * phi[phase] * (summed - square[phase])
            - 6.0 * phi[phase] * (1.0 - phi[phase]) * psi
        )
        rates.append(rate)
    mean_rate = (rates[0] + rates[1] + rates[2] + rates[3]) * 0.25
    return jnp.stack([phi[phase] + DT * (rates[phase] - mean_rate) for phase in range(4)])


def shape_fn(values):
    return values * values * (3.0 - 2.0 * values)


def chem_update(fields, side, phi_old, phi_new):
    chem = fields[4:]
    centre_d = DSOL + (DLIQ - DSOL) * fields[0]
    side_d = [DSOL + (DLIQ - DSOL) * s[0] for s in side]
    side_m = [s[4:] for s in side]
    flux = jnp.zeros_like(chem)
    for way in range(6):
        flux = flux + 0.5 * (centre_d + side_d[way]) * (side_m[way] - chem)
    delta = shape_fn(phi_new) - shape_fn(phi_old)
    result = []
    for comp in range(2):
        change = (
            COMP[0][comp] * delta[0]
            + COMP[1][comp] * delta[1]
            + COMP[2][comp] * delta[2]
            + COMP[3][comp] * delta[3]
        )
        result.append(chem[comp] + DT * flux[comp] - change)
    return jnp.stack(result)


def shards(labels, mu_start, front_blocks):
    cells_x, cells_y, cells_z = labels.shape
    lift = cells_z // 4
    bricks_y = lax.axis_size("gy")
    bricks_z = lax.axis_size("gz")
    depth = cells_z * bricks_z
    index_x = lax.axis_index("gx")
    index_y = lax.axis_index("gy")
    index_z = lax.axis_index("gz")
    bottom_brick = index_z == 0
    top_brick = index_z == bricks_z - 1
    base_z = index_z * cells_z
    rim_y = 4

    in_column = front_blocks[:, 0] == index_x

    def active(ypos, zpos):
        brick_y = (index_y + jnp.floor_divide(ypos, cells_y)) % bricks_y
        block = jnp.floor_divide(zpos, BZ)
        hits = (
            in_column[:, None, None]
            & (front_blocks[:, 1][:, None, None] == brick_y[None, :, None])
            & (front_blocks[:, 2][:, None, None] == block[None, None, :])
        )
        return jnp.any(hits, 0)

    low = lift - 4
    count = lift + 4
    stride = cells_z - low + count
    lane_z = jnp.arange(stride, dtype=jnp.int32)
    under_z = base_z + low + lane_z

    def step(ext, first_y, zpos, offset):
        size = ext.shape[2] - 2 * stride
        fields = ext[..., stride : stride + size]
        nrows = size // stride
        ypos = first_y + jnp.arange(nrows, dtype=jnp.int32)
        xlo, xhi = x_halos(fields)
        side = neighbours(ext, xlo, xhi, stride)
        on = active(ypos, zpos).reshape(-1)
        zflat = jnp.tile(under_z, nrows)
        phi_new = jnp.where(
            on[None, None],
            phase_update(fields, side, zflat, 0, depth),
            fields[:4],
        )
        mu_new = chem_update(fields, side, fields[:4], phi_new)
        return jnp.concatenate([phi_new, mu_new], 0)

    def lane_index(ext):
        return lax.broadcasted_iota(jnp.int32, ext.shape, 2) % stride

    def edge_at(ext, at, cond):
        up = jnp.concatenate([ext[..., :1], ext[..., :-1]], 2)
        return jnp.where(cond & (lane_index(ext) == at), up, ext)

    def edge_below(ext, at, cond):
        down = jnp.concatenate([ext[..., 1:], ext[..., -1:]], 2)
        return jnp.where(cond & (lane_index(ext) == at), down, ext)

    start = jnp.concatenate([labels.astype(jnp.float32)[None], mu_start], 0)
    nf = 4 + mu_start.shape[0]
    below_y = lax.ppermute(start[:, :, -rim_y:], "gy", ring("gy", 1))
    above_y = lax.ppermute(start[:, :, :rim_y], "gy", ring("gy", -1))
    wide = jnp.concatenate([below_y, start, above_y], 2)

    above = lax.ppermute(wide[..., :count].reshape(wide.shape[0], -1), "gz", line("gz", -1))
    def expand(part):
        return jnp.concatenate(
            [jnp.stack([(part[0] == phase).astype(jnp.float32) for phase in range(4)]), part[1:]], 0
        )

    own = lax.optimization_barrier(expand(wide[..., low:]))
    ext = jnp.concatenate([own, expand(above.reshape(wide.shape[:3] + (count,)))], 3)
    rows = ext.shape[2]
    ext = ext.reshape(ext.shape[0], ext.shape[1], rows * stride)
    pre_z = base_z + low + lane_z
    post_z = pre_z - lift
    ext = edge_at(ext, cells_z - low, top_brick)
    ext = step(ext, 1 - rim_y, pre_z, 0)
    ext = edge_at(ext, cells_z - low, top_brick)
    ext = step(ext, 2 - rim_y, pre_z, 0)
    liquid = jnp.where(lax.broadcasted_iota(jnp.int32, ext.shape, 0) == 0, 1.0, 0.0).astype(jnp.float32)
    ext = jnp.where(top_brick & (lane_index(ext) >= cells_z - low), liquid, ext)
    ext = edge_below(ext, lift - low - 1, bottom_brick)
    ext = edge_at(ext, cells_z + lift - low, top_brick)
    ext = step(ext, 3 - rim_y, post_z, lift)
    ext = edge_below(ext, lift - low - 1, bottom_brick)
    ext = edge_at(ext, cells_z + lift - low, top_brick)
    grid = ext.reshape(nf, cells_x, cells_y + 2, stride)
    first = lift - low
    fields = grid[:, :, 1:-1, first : first + cells_z]
    xlo, xhi = x_halos(fields)
    side = [
        jnp.concatenate([fields[:, 1:], xhi[:, None]], 1),
        jnp.concatenate([xlo[:, None], fields[:, :-1]], 1),
        grid[:, :, 2:, first : first + cells_z],
        grid[:, :, :-2, first : first + cells_z],
        grid[:, :, 1:-1, first + 1 : first + 1 + cells_z],
        grid[:, :, 1:-1, first - 1 : first - 1 + cells_z],
    ]
    ypos = jnp.arange(cells_y, dtype=jnp.int32)
    zlast = post_z[first : first + cells_z]
    phi_new = jnp.where(
        active(ypos, zlast)[None, None],
        phase_update(fields, side, under_z[first : first + cells_z], 0, depth),
        fields[:4],
    )
    mu_new = chem_update(fields, side, fields[:4], phi_new)
    return (phi_new, mu_new)


def solution(mesh):
    placed = (P("gx", "gy", "gz"), P(None, "gx", "gy", "gz"), P())
    return jax.shard_map(
        shards,
        mesh=mesh,
        in_specs=placed,
        out_specs=(P(None, "gx", "gy", "gz"), P(None, "gx", "gy", "gz")),
        check_vma=False,
    )
```

```python
import jax
import jax.numpy as jnp
from jax import lax
from jax.sharding import PartitionSpec as P

BZ = 16


COMP = ((0.0, 0.0), (1.0, -0.5), (-0.5, 1.0), (-0.5, -0.5))
LATENT = (0.0, 1.0, 1.0, 1.0)
DT = 0.05
KAPPA = 1.5
WELL = 12.0
DLIQ = 3.0
DSOL = 0.3


def ring(axis, by):
    count = lax.axis_size(axis)
    return [(i, (i + by) % count) for i in range(count)]


def line(axis, by):
    count = lax.axis_size(axis)
    return [(i, i + by) for i in range(count) if 0 <= i + by < count]


def x_halos(block):
    if lax.axis_size("gx") == 2:
        pair = jnp.stack([block[:, -1], block[:, 0]])
        got = lax.ppermute(pair, "gx", ring("gx", 1))
        return got[0], got[1]
    xlo = lax.ppermute(block[:, -1], "gx", ring("gx", 1))
    xhi = lax.ppermute(block[:, 0], "gx", ring("gx", -1))
    return xlo, xhi


def neighbours(ext, xlo, xhi, stride):
    size = ext.shape[2] - 2 * stride
    fields = ext[..., stride : stride + size]
    return [
        jnp.concatenate([fields[:, 1:], xhi[:, None]], 1),
        jnp.concatenate([xlo[:, None], fields[:, :-1]], 1),
        ext[..., 2 * stride :],
        ext[..., :size],
        ext[..., stride + 1 : stride + 1 + size],
        ext[..., stride - 1 : stride - 1 + size],
    ]


def phase_update(fields, side, zglob, offset, depth):
    phi = fields[:4]
    chem = fields[4:]
    beside_all = [s[:4] for s in side]
    total = (
        beside_all[0]
        + beside_all[1]
        + beside_all[2]
        + beside_all[3]
        + beside_all[4]
        + beside_all[5]
    )
    lap = total - 6.0 * phi
    square = phi * phi
    summed = square[0] + square[1] + square[2] + square[3]
    under = 2.0 * ((zglob + offset).astype(jnp.float32) / depth - 0.5)
    rates = []
    for phase in range(4):
        psi = -(COMP[phase][0] * chem[0] + COMP[phase][1] * chem[1]) + LATENT[phase] * under
        rate = (
            KAPPA * lap[phase]
            - WELL * phi[phase] * (summed - square[phase])
            - 6.0 * phi[phase] * (1.0 - phi[phase]) * psi
        )
        rates.append(rate)
    mean_rate = (rates[0] + rates[1] + rates[2] + rates[3]) * 0.25
    return jnp.stack([phi[phase] + DT * (rates[phase] - mean_rate) for phase in range(4)])


def shape_fn(values):
    return values * values * (3.0 - 2.0 * values)


def chem_update(fields, side, phi_old, phi_new):
    chem = fields[4:]
    centre_d = DSOL + (DLIQ - DSOL) * fields[0]
    side_d = [DSOL + (DLIQ - DSOL) * s[0] for s in side]
    side_m = [s[4:] for s in side]
    flux = jnp.zeros_like(chem)
    for way in range(6):
        flux = flux + 0.5 * (centre_d + side_d[way]) * (side_m[way] - chem)
    delta = shape_fn(phi_new) - shape_fn(phi_old)
    result = []
    for comp in range(2):
        change = (
            COMP[0][comp] * delta[0]
            + COMP[1][comp] * delta[1]
            + COMP[2][comp] * delta[2]
            + COMP[3][comp] * delta[3]
        )
        result.append(chem[comp] + DT * flux[comp] - change)
    return jnp.stack(result)


def shards(labels, mu_start, front_blocks):
    cells_x, cells_y, cells_z = labels.shape
    lift = cells_z // 4
    bricks_y = lax.axis_size("gy")
    bricks_z = lax.axis_size("gz")
    depth = cells_z * bricks_z
    index_x = lax.axis_index("gx")
    index_y = lax.axis_index("gy")
    index_z = lax.axis_index("gz")
    bottom_brick = index_z == 0
    top_brick = index_z == bricks_z - 1
    base_z = index_z * cells_z
    rim_y = 4

    in_column = front_blocks[:, 0] == index_x

    def active(ypos, zpos):
        brick_y = (index_y + jnp.floor_divide(ypos, cells_y)) % bricks_y
        block = jnp.floor_divide(zpos, BZ)
        hits = (
            in_column[:, None, None]
            & (front_blocks[:, 1][:, None, None] == brick_y[None, :, None])
            & (front_blocks[:, 2][:, None, None] == block[None, None, :])
        )
        return jnp.any(hits, 0)

    low = lift - 4
    count = lift + 4
    stride = cells_z - low + count
    lane_z = jnp.arange(stride, dtype=jnp.int32)
    under_z = base_z + low + lane_z

    def step(ext, first_y, zpos, offset):
        size = ext.shape[2] - 2 * stride
        fields = ext[..., stride : stride + size]
        nrows = size // stride
        ypos = first_y + jnp.arange(nrows, dtype=jnp.int32)
        xlo, xhi = x_halos(fields)
        side = neighbours(ext, xlo, xhi, stride)
        on = active(ypos, zpos).reshape(-1)
        zflat = jnp.tile(under_z, nrows)
        phi_new = jnp.where(
            on[None, None],
            phase_update(fields, side, zflat, 0, depth),
            fields[:4],
        )
        mu_new = chem_update(fields, side, fields[:4], phi_new)
        return jnp.concatenate([phi_new, mu_new], 0)

    def lane_index(ext):
        return lax.broadcasted_iota(jnp.int32, ext.shape, 2) % stride

    def edge_at(ext, at, cond):
        up = jnp.concatenate([ext[..., :1], ext[..., :-1]], 2)
        return jnp.where(cond & (lane_index(ext) == at), up, ext)

    def edge_below(ext, at, cond):
        down = jnp.concatenate([ext[..., 1:], ext[..., -1:]], 2)
        return jnp.where(cond & (lane_index(ext) == at), down, ext)

    start = jnp.concatenate([labels.astype(jnp.float32)[None], mu_start], 0)
    nf = 4 + mu_start.shape[0]
    def rows_of(lo, hi):
        return jnp.concatenate([labels[:, lo:hi].astype(jnp.float32)[None], mu_start[:, :, lo:hi]], 0)

    below_y = lax.ppermute(rows_of(cells_y - rim_y, cells_y), "gy", ring("gy", 1))
    above_y = lax.ppermute(rows_of(0, rim_y), "gy", ring("gy", -1))
    wide = jnp.concatenate([below_y, start, above_y], 2)

    above = lax.ppermute(wide[..., :count].reshape(wide.shape[0], -1), "gz", line("gz", -1))
    ext = jnp.concatenate([wide[..., low:], above.reshape(wide.shape[:3] + (count,))], 3)
    ext = jnp.concatenate(
        [jnp.stack([(ext[0] == phase).astype(jnp.float32) for phase in range(4)]), ext[1:]], 0
    )
    rows = ext.shape[2]
    ext = ext.reshape(ext.shape[0], ext.shape[1], rows * stride)
    pre_z = base_z + low + lane_z
    post_z = pre_z - lift
    ext = edge_at(ext, cells_z - low, top_brick)
    ext = step(ext, 1 - rim_y, pre_z, 0)
    ext = edge_at(ext, cells_z - low, top_brick)
    ext = step(ext, 2 - rim_y, pre_z, 0)
    liquid = jnp.where(lax.broadcasted_iota(jnp.int32, ext.shape, 0) == 0, 1.0, 0.0).astype(jnp.float32)
    ext = jnp.where(top_brick & (lane_index(ext) >= cells_z - low), liquid, ext)
    ext = edge_below(ext, lift - low - 1, bottom_brick)
    ext = edge_at(ext, cells_z + lift - low, top_brick)
    ext = step(ext, 3 - rim_y, post_z, lift)
    ext = edge_below(ext, lift - low - 1, bottom_brick)
    ext = edge_at(ext, cells_z + lift - low, top_brick)
    grid = ext.reshape(nf, cells_x, cells_y + 2, stride)
    first = lift - low
    fields = grid[:, :, 1:-1, first : first + cells_z]
    xlo, xhi = x_halos(fields)
    side = [
        jnp.concatenate([fields[:, 1:], xhi[:, None]], 1),
        jnp.concatenate([xlo[:, None], fields[:, :-1]], 1),
        grid[:, :, 2:, first : first + cells_z],
        grid[:, :, :-2, first : first + cells_z],
        grid[:, :, 1:-1, first + 1 : first + 1 + cells_z],
        grid[:, :, 1:-1, first - 1 : first - 1 + cells_z],
    ]
    ypos = jnp.arange(cells_y, dtype=jnp.int32)
    zlast = post_z[first : first + cells_z]
    phi_new = jnp.where(
        active(ypos, zlast)[None, None],
        phase_update(fields, side, under_z[first : first + cells_z], 0, depth),
        fields[:4],
    )
    mu_new = chem_update(fields, side, fields[:4], phi_new)
    return (phi_new, mu_new)


def solution(mesh):
    placed = (P("gx", "gy", "gz"), P(None, "gx", "gy", "gz"), P())
    return jax.shard_map(
        shards,
        mesh=mesh,
        in_specs=placed,
        out_specs=(P(None, "gx", "gy", "gz"), P(None, "gx", "gy", "gz")),
        check_vma=False,
    )
```

```python
import jax
import jax.numpy as jnp
from jax import lax
from jax.sharding import PartitionSpec as P

BZ = 16


COMP = ((0.0, 0.0), (1.0, -0.5), (-0.5, 1.0), (-0.5, -0.5))
LATENT = (0.0, 1.0, 1.0, 1.0)
DT = 0.05
KAPPA = 1.5
WELL = 12.0
DLIQ = 3.0
DSOL = 0.3


def ring(axis, by):
    count = lax.axis_size(axis)
    return [(i, (i + by) % count) for i in range(count)]


def line(axis, by):
    count = lax.axis_size(axis)
    return [(i, i + by) for i in range(count) if 0 <= i + by < count]


def x_halos(block):
    if lax.axis_size("gx") == 2:
        pair = jnp.stack([block[:, -1], block[:, 0]])
        got = lax.ppermute(pair, "gx", ring("gx", 1))
        return got[0], got[1]
    xlo = lax.ppermute(block[:, -1], "gx", ring("gx", 1))
    xhi = lax.ppermute(block[:, 0], "gx", ring("gx", -1))
    return xlo, xhi


def neighbours(ext, xlo, xhi, stride):
    size = ext.shape[2] - 2 * stride
    fields = ext[..., stride : stride + size]
    return [
        jnp.concatenate([fields[:, 1:], xhi[:, None]], 1),
        jnp.concatenate([xlo[:, None], fields[:, :-1]], 1),
        ext[..., 2 * stride :],
        ext[..., :size],
        ext[..., stride + 1 : stride + 1 + size],
        ext[..., stride - 1 : stride - 1 + size],
    ]


def phase_update(fields, side, zglob, offset, depth):
    phi = fields[:4]
    chem = fields[4:]
    beside_all = [s[:4] for s in side]
    total = (
        beside_all[0]
        + beside_all[1]
        + beside_all[2]
        + beside_all[3]
        + beside_all[4]
        + beside_all[5]
    )
    lap = total - 6.0 * phi
    square = phi * phi
    summed = square[0] + square[1] + square[2] + square[3]
    under = 2.0 * ((zglob + offset).astype(jnp.float32) / depth - 0.5)
    rates = []
    for phase in range(4):
        psi = -(COMP[phase][0] * chem[0] + COMP[phase][1] * chem[1]) + LATENT[phase] * under
        rate = (
            KAPPA * lap[phase]
            - WELL * phi[phase] * (summed - square[phase])
            - 6.0 * phi[phase] * (1.0 - phi[phase]) * psi
        )
        rates.append(rate)
    mean_rate = (rates[0] + rates[1] + rates[2] + rates[3]) * 0.25
    return jnp.stack([phi[phase] + DT * (rates[phase] - mean_rate) for phase in range(4)])


def shape_fn(values):
    return values * values * (3.0 - 2.0 * values)


def chem_update(fields, side, phi_old, phi_new):
    chem = fields[4:]
    centre_d = DSOL + (DLIQ - DSOL) * fields[0]
    side_d = [DSOL + (DLIQ - DSOL) * s[0] for s in side]
    side_m = [s[4:] for s in side]
    flux = jnp.zeros_like(chem)
    for way in range(6):
        flux = flux + 0.5 * (centre_d + side_d[way]) * (side_m[way] - chem)
    delta = shape_fn(phi_new) - shape_fn(phi_old)
    result = []
    for comp in range(2):
        change = (
            COMP[0][comp] * delta[0]
            + COMP[1][comp] * delta[1]
            + COMP[2][comp] * delta[2]
            + COMP[3][comp] * delta[3]
        )
        result.append(chem[comp] + DT * flux[comp] - change)
    return jnp.stack(result)


def shards(labels, mu_start, front_blocks):
    cells_x, cells_y, cells_z = labels.shape
    lift = cells_z // 4
    bricks_y = lax.axis_size("gy")
    bricks_z = lax.axis_size("gz")
    depth = cells_z * bricks_z
    index_x = lax.axis_index("gx")
    index_y = lax.axis_index("gy")
    index_z = lax.axis_index("gz")
    bottom_brick = index_z == 0
    top_brick = index_z == bricks_z - 1
    base_z = index_z * cells_z
    rim_y = 4

    in_column = front_blocks[:, 0] == index_x

    def active(ypos, zpos):
        brick_y = (index_y + jnp.floor_divide(ypos, cells_y)) % bricks_y
        block = jnp.floor_divide(zpos, BZ)
        hits = (
            in_column[:, None, None]
            & (front_blocks[:, 1][:, None, None] == brick_y[None, :, None])
            & (front_blocks[:, 2][:, None, None] == block[None, None, :])
        )
        return jnp.any(hits, 0)

    low = lift - 4
    count = lift + 4
    stride = cells_z - low + count
    lane_z = jnp.arange(stride, dtype=jnp.int32)
    under_z = base_z + low + lane_z

    def step(ext, first_y, zpos, offset):
        size = ext.shape[2] - 2 * stride
        fields = ext[..., stride : stride + size]
        nrows = size // stride
        ypos = first_y + jnp.arange(nrows, dtype=jnp.int32)
        xlo, xhi = x_halos(fields)
        side = neighbours(ext, xlo, xhi, stride)
        on = active(ypos, zpos).reshape(-1)
        zflat = jnp.tile(under_z, nrows)
        phi_new = jnp.where(
            on[None, None],
            phase_update(fields, side, zflat, 0, depth),
            fields[:4],
        )
        mu_new = chem_update(fields, side, fields[:4], phi_new)
        return jnp.concatenate([phi_new, mu_new], 0)

    def lane_index(ext):
        return lax.broadcasted_iota(jnp.int32, ext.shape, 2) % stride

    def edge_at(ext, at, cond):
        up = jnp.concatenate([ext[..., :1], ext[..., :-1]], 2)
        return jnp.where(cond & (lane_index(ext) == at), up, ext)

    def edge_below(ext, at, cond):
        down = jnp.concatenate([ext[..., 1:], ext[..., -1:]], 2)
        return jnp.where(cond & (lane_index(ext) == at), down, ext)

    start = jnp.concatenate([labels.astype(jnp.float32)[None], mu_start], 0)
    nf = 4 + mu_start.shape[0]
    below_y = lax.ppermute(start[:, :, -rim_y:], "gy", ring("gy", 1))
    above_y = lax.ppermute(start[:, :, :rim_y], "gy", ring("gy", -1))
    wide = jnp.concatenate([below_y, start, above_y], 2)

    above = lax.ppermute(wide[..., :count].reshape(wide.shape[0], -1), "gz", line("gz", -1))
    ext = jnp.concatenate([wide[..., low:], above.reshape(wide.shape[:3] + (count,))], 3)
    ext = jnp.concatenate(
        [jnp.stack([(ext[0] == phase).astype(jnp.float32) for phase in range(4)]), ext[1:]], 0
    )
    rows = ext.shape[2]
    ext = ext.reshape(ext.shape[0], ext.shape[1], rows * stride)
    pre_z = base_z + low + lane_z
    post_z = pre_z - lift
    def fixes(ext, below_at=None, above_at=None, liquid_from=None):
        lane = lane_index(ext)
        if liquid_from is not None:
            liquid = jnp.where(lax.broadcasted_iota(jnp.int32, ext.shape, 0) == 0, 1.0, 0.0)
            ext = jnp.where(top_brick & (lane >= liquid_from), liquid.astype(jnp.float32), ext)
        out = ext
        if below_at is not None:
            down = jnp.concatenate([ext[..., 1:], ext[..., -1:]], 2)
            out = jnp.where(bottom_brick & (lane == below_at), down, out)
        if above_at is not None:
            up = jnp.concatenate([ext[..., :1], ext[..., :-1]], 2)
            out = jnp.where(top_brick & (lane == above_at), up, out)
        return out

    ext = fixes(ext, above_at=cells_z - low)
    ext = step(ext, 1 - rim_y, pre_z, 0)
    ext = fixes(ext, above_at=cells_z - low)
    ext = step(ext, 2 - rim_y, pre_z, 0)
    ext = fixes(ext, lift - low - 1, cells_z + lift - low, cells_z - low)
    ext = step(ext, 3 - rim_y, post_z, lift)
    ext = fixes(ext, lift - low - 1, cells_z + lift - low)
    grid = ext.reshape(nf, cells_x, cells_y + 2, stride)
    first = lift - low
    fields = grid[:, :, 1:-1, first : first + cells_z]
    xlo, xhi = x_halos(fields)
    side = [
        jnp.concatenate([fields[:, 1:], xhi[:, None]], 1),
        jnp.concatenate([xlo[:, None], fields[:, :-1]], 1),
        grid[:, :, 2:, first : first + cells_z],
        grid[:, :, :-2, first : first + cells_z],
        grid[:, :, 1:-1, first + 1 : first + 1 + cells_z],
        grid[:, :, 1:-1, first - 1 : first - 1 + cells_z],
    ]
    ypos = jnp.arange(cells_y, dtype=jnp.int32)
    zlast = post_z[first : first + cells_z]
    phi_new = jnp.where(
        active(ypos, zlast)[None, None],
        phase_update(fields, side, under_z[first : first + cells_z], 0, depth),
        fields[:4],
    )
    mu_new = chem_update(fields, side, fields[:4], phi_new)
    return (phi_new, mu_new)


def solution(mesh):
    placed = (P("gx", "gy", "gz"), P(None, "gx", "gy", "gz"), P())
    return jax.shard_map(
        shards,
        mesh=mesh,
        in_specs=placed,
        out_specs=(P(None, "gx", "gy", "gz"), P(None, "gx", "gy", "gz")),
        check_vma=False,
    )
```

```python
import jax
import jax.numpy as jnp
from jax import lax
from jax.sharding import PartitionSpec as P

BZ = 16


COMP = ((0.0, 0.0), (1.0, -0.5), (-0.5, 1.0), (-0.5, -0.5))
LATENT = (0.0, 1.0, 1.0, 1.0)
DT = 0.05
KAPPA = 1.5
WELL = 12.0
DLIQ = 3.0
DSOL = 0.3


def ring(axis, by):
    count = lax.axis_size(axis)
    return [(i, (i + by) % count) for i in range(count)]


def line(axis, by):
    count = lax.axis_size(axis)
    return [(i, i + by) for i in range(count) if 0 <= i + by < count]


def x_halos(block):
    if lax.axis_size("gx") == 2:
        pair = jnp.stack([block[:, -1], block[:, 0]])
        got = lax.ppermute(pair, "gx", ring("gx", 1))
        return got[0], got[1]
    xlo = lax.ppermute(block[:, -1], "gx", ring("gx", 1))
    xhi = lax.ppermute(block[:, 0], "gx", ring("gx", -1))
    return xlo, xhi


def neighbours(ext, xlo, xhi, stride):
    size = ext.shape[2] - 2 * stride
    fields = ext[..., stride : stride + size]
    return [
        jnp.concatenate([fields[:, 1:], xhi[:, None]], 1),
        jnp.concatenate([xlo[:, None], fields[:, :-1]], 1),
        ext[..., 2 * stride :],
        ext[..., :size],
        ext[..., stride + 1 : stride + 1 + size],
        ext[..., stride - 1 : stride - 1 + size],
    ]


def phase_update(fields, side, zglob, offset, depth):
    phi = fields[:4]
    chem = fields[4:]
    beside_all = [s[:4] for s in side]
    total = (
        beside_all[0]
        + beside_all[1]
        + beside_all[2]
        + beside_all[3]
        + beside_all[4]
        + beside_all[5]
    )
    lap = total - 6.0 * phi
    square = phi * phi
    summed = square[0] + square[1] + square[2] + square[3]
    under = 2.0 * ((zglob + offset).astype(jnp.float32) / depth - 0.5)
    rates = []
    for phase in range(4):
        psi = -(COMP[phase][0] * chem[0] + COMP[phase][1] * chem[1]) + LATENT[phase] * under
        rate = (
            KAPPA * lap[phase]
            - WELL * phi[phase] * (summed - square[phase])
            - 6.0 * phi[phase] * (1.0 - phi[phase]) * psi
        )
        rates.append(rate)
    mean_rate = (rates[0] + rates[1] + rates[2] + rates[3]) * 0.25
    return jnp.stack([phi[phase] + DT * (rates[phase] - mean_rate) for phase in range(4)])


def shape_fn(values):
    return values * values * (3.0 - 2.0 * values)


def chem_update(fields, side, phi_old, phi_new):
    chem = fields[4:]
    centre_d = DSOL + (DLIQ - DSOL) * fields[0]
    side_d = [DSOL + (DLIQ - DSOL) * s[0] for s in side]
    side_m = [s[4:] for s in side]
    flux = jnp.zeros_like(chem)
    for way in range(6):
        flux = flux + 0.5 * (centre_d + side_d[way]) * (side_m[way] - chem)
    delta = shape_fn(phi_new) - shape_fn(phi_old)
    result = []
    for comp in range(2):
        change = (
            COMP[0][comp] * delta[0]
            + COMP[1][comp] * delta[1]
            + COMP[2][comp] * delta[2]
            + COMP[3][comp] * delta[3]
        )
        result.append(chem[comp] + DT * flux[comp] - change)
    return jnp.stack(result)


def shards(labels, mu_start, front_blocks):
    cells_x, cells_y, cells_z = labels.shape
    lift = cells_z // 4
    bricks_y = lax.axis_size("gy")
    bricks_z = lax.axis_size("gz")
    depth = cells_z * bricks_z
    index_x = lax.axis_index("gx")
    index_y = lax.axis_index("gy")
    index_z = lax.axis_index("gz")
    bottom_brick = index_z == 0
    top_brick = index_z == bricks_z - 1
    base_z = index_z * cells_z
    rim_y = 4

    in_column = front_blocks[:, 0] == index_x

    def active(ypos, zpos):
        brick_y = (index_y + jnp.floor_divide(ypos, cells_y)) % bricks_y
        block = jnp.floor_divide(zpos, BZ)
        hits = (
            in_column[:, None, None]
            & (front_blocks[:, 1][:, None, None] == brick_y[None, :, None])
            & (front_blocks[:, 2][:, None, None] == block[None, None, :])
        )
        return jnp.any(hits, 0)

    low = lift - 4
    count = lift + 4
    stride = cells_z - low + count
    lane_z = jnp.arange(stride, dtype=jnp.int32)
    under_z = base_z + low + lane_z

    def step(ext, first_y, zpos, offset):
        size = ext.shape[2] - 2 * stride
        fields = ext[..., stride : stride + size]
        nrows = size // stride
        ypos = first_y + jnp.arange(nrows, dtype=jnp.int32)
        xlo, xhi = x_halos(fields)
        side = neighbours(ext, xlo, xhi, stride)
        on = active(ypos, zpos).reshape(-1)
        zflat = jnp.tile(under_z, nrows)
        phi_new = jnp.where(
            on[None, None],
            phase_update(fields, side, zflat, 0, depth),
            fields[:4],
        )
        mu_new = chem_update(fields, side, fields[:4], phi_new)
        return jnp.concatenate([phi_new, mu_new], 0)

    def lane_index(ext):
        return lax.broadcasted_iota(jnp.int32, ext.shape, 2) % stride

    def edge_at(ext, at, cond):
        up = jnp.concatenate([ext[..., :1], ext[..., :-1]], 2)
        return jnp.where(cond & (lane_index(ext) == at), up, ext)

    def edge_below(ext, at, cond):
        down = jnp.concatenate([ext[..., 1:], ext[..., -1:]], 2)
        return jnp.where(cond & (lane_index(ext) == at), down, ext)

    start = jnp.concatenate([labels.astype(jnp.float32)[None], mu_start], 0)
    nf = 4 + mu_start.shape[0]
    below_y = lax.ppermute(start[:, :, -rim_y:], "gy", ring("gy", 1))
    above_y = lax.ppermute(start[:, :, :rim_y], "gy", ring("gy", -1))
    wide = jnp.concatenate([below_y, start, above_y], 2)

    bricks_yz = bricks_y * bricks_z

    def diagonal(by):
        pairs = []
        for source in range(bricks_yz):
            sy, sz = source // bricks_z, source % bricks_z
            if sz >= 1:
                pairs.append((source, ((sy + by) % bricks_y) * bricks_z + sz - 1))
        return pairs

    def flat_top(part):
        return part[..., :count].reshape(part.shape[0], -1)

    top_own = lax.ppermute(flat_top(start), "gz", line("gz", -1))
    top_low = lax.ppermute(flat_top(start[:, :, -rim_y:]), ("gy", "gz"), diagonal(1))
    top_high = lax.ppermute(flat_top(start[:, :, :rim_y]), ("gy", "gz"), diagonal(-1))
    cells_xs = start.shape[:2]
    above = jnp.concatenate(
        [
            top_low.reshape(cells_xs + (rim_y, count)),
            top_own.reshape(cells_xs + (cells_y, count)),
            top_high.reshape(cells_xs + (rim_y, count)),
        ],
        2,
    )
    ext = jnp.concatenate([wide[..., low:], above], 3)
    ext = jnp.concatenate(
        [jnp.stack([(ext[0] == phase).astype(jnp.float32) for phase in range(4)]), ext[1:]], 0
    )
    rows = ext.shape[2]
    ext = ext.reshape(ext.shape[0], ext.shape[1], rows * stride)
    pre_z = base_z + low + lane_z
    post_z = pre_z - lift
    def fixes(ext, below_at=None, above_at=None, liquid_from=None):
        lane = lane_index(ext)
        if liquid_from is not None:
            liquid = jnp.where(lax.broadcasted_iota(jnp.int32, ext.shape, 0) == 0, 1.0, 0.0)
            ext = jnp.where(top_brick & (lane >= liquid_from), liquid.astype(jnp.float32), ext)
        out = ext
        if below_at is not None:
            down = jnp.concatenate([ext[..., 1:], ext[..., -1:]], 2)
            out = jnp.where(bottom_brick & (lane == below_at), down, out)
        if above_at is not None:
            up = jnp.concatenate([ext[..., :1], ext[..., :-1]], 2)
            out = jnp.where(top_brick & (lane == above_at), up, out)
        return out

    ext = fixes(ext, above_at=cells_z - low)
    ext = step(ext, 1 - rim_y, pre_z, 0)
    ext = fixes(ext, above_at=cells_z - low)
    ext = step(ext, 2 - rim_y, pre_z, 0)
    ext = fixes(ext, lift - low - 1, cells_z + lift - low, cells_z - low)
    ext = step(ext, 3 - rim_y, post_z, lift)
    ext = fixes(ext, lift - low - 1, cells_z + lift - low)
    grid = ext.reshape(nf, cells_x, cells_y + 2, stride)
    first = lift - low
    fields = grid[:, :, 1:-1, first : first + cells_z]
    xlo, xhi = x_halos(fields)
    side = [
        jnp.concatenate([fields[:, 1:], xhi[:, None]], 1),
        jnp.concatenate([xlo[:, None], fields[:, :-1]], 1),
        grid[:, :, 2:, first : first + cells_z],
        grid[:, :, :-2, first : first + cells_z],
        grid[:, :, 1:-1, first + 1 : first + 1 + cells_z],
        grid[:, :, 1:-1, first - 1 : first - 1 + cells_z],
    ]
    ypos = jnp.arange(cells_y, dtype=jnp.int32)
    zlast = post_z[first : first + cells_z]
    phi_new = jnp.where(
        active(ypos, zlast)[None, None],
        phase_update(fields, side, under_z[first : first + cells_z], 0, depth),
        fields[:4],
    )
    mu_new = chem_update(fields, side, fields[:4], phi_new)
    return (phi_new, mu_new)


def solution(mesh):
    placed = (P("gx", "gy", "gz"), P(None, "gx", "gy", "gz"), P())
    return jax.shard_map(
        shards,
        mesh=mesh,
        in_specs=placed,
        out_specs=(P(None, "gx", "gy", "gz"), P(None, "gx", "gy", "gz")),
        check_vma=False,
    )
```

```python
import jax
import jax.numpy as jnp
from jax import lax
from jax.sharding import PartitionSpec as P

BZ = 16


COMP = ((0.0, 0.0), (1.0, -0.5), (-0.5, 1.0), (-0.5, -0.5))
LATENT = (0.0, 1.0, 1.0, 1.0)
DT = 0.05
KAPPA = 1.5
WELL = 12.0
DLIQ = 3.0
DSOL = 0.3


def ring(axis, by):
    count = lax.axis_size(axis)
    return [(i, (i + by) % count) for i in range(count)]


def line(axis, by):
    count = lax.axis_size(axis)
    return [(i, i + by) for i in range(count) if 0 <= i + by < count]


def x_halos(block):
    if lax.axis_size("gx") == 2:
        pair = jnp.stack([block[:, -1], block[:, 0]])
        got = lax.ppermute(pair, "gx", ring("gx", 1))
        return got[0], got[1]
    xlo = lax.ppermute(block[:, -1], "gx", ring("gx", 1))
    xhi = lax.ppermute(block[:, 0], "gx", ring("gx", -1))
    return xlo, xhi


def neighbours(ext, xlo, xhi, stride):
    size = ext.shape[2] - 2 * stride
    fields = ext[..., stride : stride + size]
    return [
        jnp.concatenate([fields[:, 1:], xhi[:, None]], 1),
        jnp.concatenate([xlo[:, None], fields[:, :-1]], 1),
        ext[..., 2 * stride :],
        ext[..., :size],
        ext[..., stride + 1 : stride + 1 + size],
        ext[..., stride - 1 : stride - 1 + size],
    ]


def phase_update(fields, side, zglob, offset, depth):
    phi = fields[:4]
    chem = fields[4:]
    beside_all = [s[:4] for s in side]
    total = (
        beside_all[0]
        + beside_all[1]
        + beside_all[2]
        + beside_all[3]
        + beside_all[4]
        + beside_all[5]
    )
    lap = total - 6.0 * phi
    square = phi * phi
    summed = square[0] + square[1] + square[2] + square[3]
    under = 2.0 * ((zglob + offset).astype(jnp.float32) / depth - 0.5)
    rates = []
    for phase in range(4):
        psi = -(COMP[phase][0] * chem[0] + COMP[phase][1] * chem[1]) + LATENT[phase] * under
        rate = (
            KAPPA * lap[phase]
            - WELL * phi[phase] * (summed - square[phase])
            - 6.0 * phi[phase] * (1.0 - phi[phase]) * psi
        )
        rates.append(rate)
    mean_rate = (rates[0] + rates[1] + rates[2] + rates[3]) * 0.25
    return jnp.stack([phi[phase] + DT * (rates[phase] - mean_rate) for phase in range(4)])


def shape_fn(values):
    return values * values * (3.0 - 2.0 * values)


def chem_update(fields, side, phi_old, phi_new):
    chem = fields[4:]
    centre_d = DSOL + (DLIQ - DSOL) * fields[0]
    side_d = [DSOL + (DLIQ - DSOL) * s[0] for s in side]
    side_m = [s[4:] for s in side]
    flux = jnp.zeros_like(chem)
    for way in range(6):
        flux = flux + 0.5 * (centre_d + side_d[way]) * (side_m[way] - chem)
    delta = shape_fn(phi_new) - shape_fn(phi_old)
    result = []
    for comp in range(2):
        change = (
            COMP[0][comp] * delta[0]
            + COMP[1][comp] * delta[1]
            + COMP[2][comp] * delta[2]
            + COMP[3][comp] * delta[3]
        )
        result.append(chem[comp] + DT * flux[comp] - change)
    return jnp.stack(result)


def shards(labels, mu_start, front_blocks):
    cells_x, cells_y, cells_z = labels.shape
    lift = cells_z // 4
    bricks_y = lax.axis_size("gy")
    bricks_z = lax.axis_size("gz")
    depth = cells_z * bricks_z
    index_x = lax.axis_index("gx")
    index_y = lax.axis_index("gy")
    index_z = lax.axis_index("gz")
    bottom_brick = index_z == 0
    top_brick = index_z == bricks_z - 1
    base_z = index_z * cells_z
    rim_y = 4

    in_column = front_blocks[:, 0] == index_x

    def active(ypos, zpos):
        brick_y = (index_y + jnp.floor_divide(ypos, cells_y)) % bricks_y
        block = jnp.floor_divide(zpos, BZ)
        hits = (
            in_column[:, None, None]
            & (front_blocks[:, 1][:, None, None] == brick_y[None, :, None])
            & (front_blocks[:, 2][:, None, None] == block[None, None, :])
        )
        return jnp.any(hits, 0)

    low = lift - 4
    count = lift + 4
    stride = cells_z - low + count
    lane_z = jnp.arange(stride, dtype=jnp.int32)
    under_z = base_z + low + lane_z

    def step(ext, first_y, zpos, offset):
        size = ext.shape[2] - 2 * stride
        fields = ext[..., stride : stride + size]
        nrows = size // stride
        ypos = first_y + jnp.arange(nrows, dtype=jnp.int32)
        xlo, xhi = x_halos(fields)
        side = neighbours(ext, xlo, xhi, stride)
        on = active(ypos, zpos).reshape(-1)
        zflat = jnp.tile(under_z, nrows)
        phi_new = jnp.where(
            on[None, None],
            phase_update(fields, side, zflat, 0, depth),
            fields[:4],
        )
        mu_new = chem_update(fields, side, fields[:4], phi_new)
        return jnp.concatenate([phi_new, mu_new], 0)

    def lane_index(ext):
        return lax.broadcasted_iota(jnp.int32, ext.shape, 2) % stride

    def edge_at(ext, at, cond):
        up = jnp.concatenate([ext[..., :1], ext[..., :-1]], 2)
        return jnp.where(cond & (lane_index(ext) == at), up, ext)

    def edge_below(ext, at, cond):
        down = jnp.concatenate([ext[..., 1:], ext[..., -1:]], 2)
        return jnp.where(cond & (lane_index(ext) == at), down, ext)

    start = jnp.concatenate([labels.astype(jnp.float32)[None], mu_start], 0)
    nf = 4 + mu_start.shape[0]
    if bricks_y > 2:
        slot = lax.broadcasted_iota(jnp.int32, (bricks_y,) + start[:, :, :rim_y].shape, 0)
        send = jnp.where(
            slot == (index_y + bricks_y - 1) % bricks_y,
            start[None, :, :, :rim_y],
            jnp.where(slot == (index_y + 1) % bricks_y, start[None, :, :, -rim_y:], 0.0),
        )
        got = lax.all_to_all(send, "gy", 0, 0)
        below_y = got[(index_y + bricks_y - 1) % bricks_y]
        above_y = got[(index_y + 1) % bricks_y]
    else:
        below_y = lax.ppermute(start[:, :, -rim_y:], "gy", ring("gy", 1))
        above_y = lax.ppermute(start[:, :, :rim_y], "gy", ring("gy", -1))
    wide = jnp.concatenate([below_y, start, above_y], 2)

    above = lax.ppermute(wide[..., :count].reshape(wide.shape[0], -1), "gz", line("gz", -1))
    ext = jnp.concatenate([wide[..., low:], above.reshape(wide.shape[:3] + (count,))], 3)
    ext = jnp.concatenate(
        [jnp.stack([(ext[0] == phase).astype(jnp.float32) for phase in range(4)]), ext[1:]], 0
    )
    rows = ext.shape[2]
    ext = ext.reshape(ext.shape[0], ext.shape[1], rows * stride)
    pre_z = base_z + low + lane_z
    post_z = pre_z - lift
    def fixes(ext, below_at=None, above_at=None, liquid_from=None):
        lane = lane_index(ext)
        if liquid_from is not None:
            liquid = jnp.where(lax.broadcasted_iota(jnp.int32, ext.shape, 0) == 0, 1.0, 0.0)
            ext = jnp.where(top_brick & (lane >= liquid_from), liquid.astype(jnp.float32), ext)
        out = ext
        if below_at is not None:
            down = jnp.concatenate([ext[..., 1:], ext[..., -1:]], 2)
            out = jnp.where(bottom_brick & (lane == below_at), down, out)
        if above_at is not None:
            up = jnp.concatenate([ext[..., :1], ext[..., :-1]], 2)
            out = jnp.where(top_brick & (lane == above_at), up, out)
        return out

    ext = fixes(ext, above_at=cells_z - low)
    ext = step(ext, 1 - rim_y, pre_z, 0)
    ext = fixes(ext, above_at=cells_z - low)
    ext = step(ext, 2 - rim_y, pre_z, 0)
    ext = fixes(ext, lift - low - 1, cells_z + lift - low, cells_z - low)
    ext = step(ext, 3 - rim_y, post_z, lift)
    ext = fixes(ext, lift - low - 1, cells_z + lift - low)
    grid = ext.reshape(nf, cells_x, cells_y + 2, stride)
    first = lift - low
    fields = grid[:, :, 1:-1, first : first + cells_z]
    xlo, xhi = x_halos(fields)
    side = [
        jnp.concatenate([fields[:, 1:], xhi[:, None]], 1),
        jnp.concatenate([xlo[:, None], fields[:, :-1]], 1),
        grid[:, :, 2:, first : first + cells_z],
        grid[:, :, :-2, first : first + cells_z],
        grid[:, :, 1:-1, first + 1 : first + 1 + cells_z],
        grid[:, :, 1:-1, first - 1 : first - 1 + cells_z],
    ]
    ypos = jnp.arange(cells_y, dtype=jnp.int32)
    zlast = post_z[first : first + cells_z]
    phi_new = jnp.where(
        active(ypos, zlast)[None, None],
        phase_update(fields, side, under_z[first : first + cells_z], 0, depth),
        fields[:4],
    )
    mu_new = chem_update(fields, side, fields[:4], phi_new)
    return (phi_new, mu_new)


def solution(mesh):
    placed = (P("gx", "gy", "gz"), P(None, "gx", "gy", "gz"), P())
    return jax.shard_map(
        shards,
        mesh=mesh,
        in_specs=placed,
        out_specs=(P(None, "gx", "gy", "gz"), P(None, "gx", "gy", "gz")),
        check_vma=False,
    )
```

```python
import jax
import jax.numpy as jnp
from jax import lax
from jax.sharding import PartitionSpec as P

BZ = 16


COMP = ((0.0, 0.0), (1.0, -0.5), (-0.5, 1.0), (-0.5, -0.5))
LATENT = (0.0, 1.0, 1.0, 1.0)
DT = 0.05
KAPPA = 1.5
WELL = 12.0
DLIQ = 3.0
DSOL = 0.3


def ring(axis, by):
    count = lax.axis_size(axis)
    return [(i, (i + by) % count) for i in range(count)]


def line(axis, by):
    count = lax.axis_size(axis)
    return [(i, i + by) for i in range(count) if 0 <= i + by < count]


def x_halos(block):
    xlo = lax.ppermute(block[:, -1], "gx", ring("gx", 1))
    xhi = lax.ppermute(block[:, 0], "gx", ring("gx", -1))
    return xlo, xhi


def neighbours(ext, xlo, xhi, stride):
    size = ext.shape[2] - 2 * stride
    fields = ext[..., stride : stride + size]
    return [
        jnp.concatenate([fields[:, 1:], xhi[:, None]], 1),
        jnp.concatenate([xlo[:, None], fields[:, :-1]], 1),
        ext[..., 2 * stride :],
        ext[..., :size],
        ext[..., stride + 1 : stride + 1 + size],
        ext[..., stride - 1 : stride - 1 + size],
    ]


def phase_update(fields, side, zglob, offset, depth):
    phi = fields[:4]
    chem = fields[4:]
    beside_all = [s[:4] for s in side]
    total = (
        beside_all[0]
        + beside_all[1]
        + beside_all[2]
        + beside_all[3]
        + beside_all[4]
        + beside_all[5]
    )
    lap = total - 6.0 * phi
    square = phi * phi
    summed = square[0] + square[1] + square[2] + square[3]
    under = 2.0 * ((zglob + offset).astype(jnp.float32) / depth - 0.5)
    rates = []
    for phase in range(4):
        psi = -(COMP[phase][0] * chem[0] + COMP[phase][1] * chem[1]) + LATENT[phase] * under
        rate = (
            KAPPA * lap[phase]
            - WELL * phi[phase] * (summed - square[phase])
            - 6.0 * phi[phase] * (1.0 - phi[phase]) * psi
        )
        rates.append(rate)
    mean_rate = (rates[0] + rates[1] + rates[2] + rates[3]) * 0.25
    return jnp.stack([phi[phase] + DT * (rates[phase] - mean_rate) for phase in range(4)])


def shape_fn(values):
    return values * values * (3.0 - 2.0 * values)


def chem_update(fields, side, phi_old, phi_new):
    chem = fields[4:]
    centre_d = DSOL + (DLIQ - DSOL) * fields[0]
    side_d = [DSOL + (DLIQ - DSOL) * s[0] for s in side]
    side_m = [s[4:] for s in side]
    flux = jnp.zeros_like(chem)
    for way in range(6):
        flux = flux + 0.5 * (centre_d + side_d[way]) * (side_m[way] - chem)
    delta = shape_fn(phi_new) - shape_fn(phi_old)
    result = []
    for comp in range(2):
        change = (
            COMP[0][comp] * delta[0]
            + COMP[1][comp] * delta[1]
            + COMP[2][comp] * delta[2]
            + COMP[3][comp] * delta[3]
        )
        result.append(chem[comp] + DT * flux[comp] - change)
    return jnp.stack(result)


def shards(labels, mu_start, front_blocks):
    cells_x, cells_y, cells_z = labels.shape
    lift = cells_z // 4
    bricks_y = lax.axis_size("gy")
    bricks_z = lax.axis_size("gz")
    depth = cells_z * bricks_z
    index_x = lax.axis_index("gx")
    index_y = lax.axis_index("gy")
    index_z = lax.axis_index("gz")
    bottom_brick = index_z == 0
    top_brick = index_z == bricks_z - 1
    base_z = index_z * cells_z
    rim_y = 4

    in_column = front_blocks[:, 0] == index_x

    def active(ypos, zpos):
        brick_y = (index_y + jnp.floor_divide(ypos, cells_y)) % bricks_y
        block = jnp.floor_divide(zpos, BZ)
        hits = (
            in_column[:, None, None]
            & (front_blocks[:, 1][:, None, None] == brick_y[None, :, None])
            & (front_blocks[:, 2][:, None, None] == block[None, None, :])
        )
        return jnp.any(hits, 0)

    low = lift - 4
    count = lift + 4
    stride = cells_z - low + count
    lane_z = jnp.arange(stride, dtype=jnp.int32)
    under_z = base_z + low + lane_z

    def step(ext, first_y, zpos, offset):
        size = ext.shape[2] - 2 * stride
        fields = ext[..., stride : stride + size]
        nrows = size // stride
        ypos = first_y + jnp.arange(nrows, dtype=jnp.int32)
        xlo, xhi = x_halos(fields)
        side = neighbours(ext, xlo, xhi, stride)
        on = active(ypos, zpos).reshape(-1)
        zflat = jnp.tile(under_z, nrows)
        phi_new = jnp.where(
            on[None, None],
            phase_update(fields, side, zflat, 0, depth),
            fields[:4],
        )
        mu_new = chem_update(fields, side, fields[:4], phi_new)
        return jnp.concatenate([phi_new, mu_new], 0)

    def lane_index(ext):
        return lax.broadcasted_iota(jnp.int32, ext.shape, 2) % stride

    def edge_at(ext, at, cond):
        up = jnp.concatenate([ext[..., :1], ext[..., :-1]], 2)
        return jnp.where(cond & (lane_index(ext) == at), up, ext)

    def edge_below(ext, at, cond):
        down = jnp.concatenate([ext[..., 1:], ext[..., -1:]], 2)
        return jnp.where(cond & (lane_index(ext) == at), down, ext)

    start = jnp.concatenate([labels.astype(jnp.float32)[None], mu_start], 0)
    nf = 4 + mu_start.shape[0]
    below_y = lax.ppermute(start[:, :, -rim_y:], "gy", ring("gy", 1))
    above_y = lax.ppermute(start[:, :, :rim_y], "gy", ring("gy", -1))
    wide = jnp.concatenate([below_y, start, above_y], 2)

    above = lax.ppermute(wide[..., :count].reshape(wide.shape[0], -1), "gz", line("gz", -1))
    ext = jnp.concatenate([wide[..., low:], above.reshape(wide.shape[:3] + (count,))], 3)
    ext = jnp.concatenate(
        [jnp.stack([(ext[0] == phase).astype(jnp.float32) for phase in range(4)]), ext[1:]], 0
    )
    rows = ext.shape[2]
    ext = ext.reshape(ext.shape[0], ext.shape[1], rows * stride)
    pre_z = base_z + low + lane_z
    post_z = pre_z - lift
    def fixes(ext, below_at=None, above_at=None, liquid_from=None):
        lane = lane_index(ext)
        if liquid_from is not None:
            liquid = jnp.where(lax.broadcasted_iota(jnp.int32, ext.shape, 0) == 0, 1.0, 0.0)
            ext = jnp.where(top_brick & (lane >= liquid_from), liquid.astype(jnp.float32), ext)
        out = ext
        if below_at is not None:
            down = jnp.concatenate([ext[..., 1:], ext[..., -1:]], 2)
            out = jnp.where(bottom_brick & (lane == below_at), down, out)
        if above_at is not None:
            up = jnp.concatenate([ext[..., :1], ext[..., :-1]], 2)
            out = jnp.where(top_brick & (lane == above_at), up, out)
        return out

    ext = fixes(ext, above_at=cells_z - low)
    ext = step(ext, 1 - rim_y, pre_z, 0)
    ext = fixes(ext, above_at=cells_z - low)
    ext = step(ext, 2 - rim_y, pre_z, 0)
    ext = fixes(ext, lift - low - 1, cells_z + lift - low, cells_z - low)
    ext = step(ext, 3 - rim_y, post_z, lift)
    ext = fixes(ext, lift - low - 1, cells_z + lift - low)
    grid = ext.reshape(nf, cells_x, cells_y + 2, stride)
    first = lift - low
    fields = grid[:, :, 1:-1, first : first + cells_z]
    xlo, xhi = x_halos(fields)
    side = [
        jnp.concatenate([fields[:, 1:], xhi[:, None]], 1),
        jnp.concatenate([xlo[:, None], fields[:, :-1]], 1),
        grid[:, :, 2:, first : first + cells_z],
        grid[:, :, :-2, first : first + cells_z],
        grid[:, :, 1:-1, first + 1 : first + 1 + cells_z],
        grid[:, :, 1:-1, first - 1 : first - 1 + cells_z],
    ]
    ypos = jnp.arange(cells_y, dtype=jnp.int32)
    zlast = post_z[first : first + cells_z]
    phi_new = jnp.where(
        active(ypos, zlast)[None, None],
        phase_update(fields, side, under_z[first : first + cells_z], 0, depth),
        fields[:4],
    )
    mu_new = chem_update(fields, side, fields[:4], phi_new)
    return (phi_new, mu_new)


def solution(mesh):
    placed = (P("gx", "gy", "gz"), P(None, "gx", "gy", "gz"), P())
    return jax.shard_map(
        shards,
        mesh=mesh,
        in_specs=placed,
        out_specs=(P(None, "gx", "gy", "gz"), P(None, "gx", "gy", "gz")),
        check_vma=False,
    )
```
